128 devices in a mesh: dp: 16 (over z, y_lo, core), tensor: 8 (over x, y_hi).
Axes of the slice: x: 4, y: 4 (y_hi: 2, y_lo: 2; y = y_hi * 2 + y_lo), z: 4, core: 2. Of those that a mesh axis runs over, the one named last changes fastest.
Arguments:
- token_ids: int32 [512], P('dp'), may hold values from 0 to 128255, as said below
- hidden_in: bfloat16 [512, 8192], P('dp'), may hold values from -6 to 6
- cotangent: bfloat16 [512, 8192], P('dp'), may hold values from -6 to 6
- gate_weight: bfloat16 [8192, 28672], P(None, ('dp', 'tensor')), may hold values from -0.0625 to 0.0625
- up_weight: bfloat16 [8192, 28672], P(None, ('dp', 'tensor')), may hold values from -0.0625 to 0.0625
- down_weight: bfloat16 [28672, 8192], P(('dp', 'tensor')), may hold values from -0.03125 to 0.03125
- gate_in_proj: bfloat16 [8192, 64], replicated, may hold values from -0.0625 to 0.0625
- up_in_proj: bfloat16 [8192, 64], replicated, may hold values from -0.0625 to 0.0625
- down_out_proj: bfloat16 [8192, 64], replicated, may hold values from -0.0625 to 0.0625
- gate_out_proj: bfloat16 [28672, 64], P(('dp', 'tensor')), may hold values from -0.03125 to 0.03125
- up_out_proj: bfloat16 [28672, 64], P(('dp', 'tensor')), may hold values from -0.03125 to 0.03125
- down_in_proj: bfloat16 [28672, 64], P(('dp', 'tensor')), may hold values from -0.03125 to 0.03125
- stored_grads: bfloat16 [4096, 12288], P(('dp', 'tensor')), may hold values from -0.0546875 to 0.0546875
- example_ids: int32 [4096], P(('dp', 'tensor')), may hold values from 0 to 1023
Outputs:
- doc_grads: bfloat16 [16, 12288], P('dp')
- example_scores: float32 [16, 1024], P(None, ('dp', 'tensor'))
The draws below stay inside these ranges and needn't reach their ends.
Inputs may be any that keep to these rules, and one draw needn't show every extreme that they name: `token_ids`: 0 marks padding, which only fills the end of a document of 32 tokens; each document has 16 or more tokens other than 0.
All inputs are finite; a program needn't handle non-finite values.
Results may differ from the reference program's by a relative error of at most 0.0051.
Values may be sent and summed in bfloat16 or wider, within the bound.
No kernel may reach another device: no remote copies, remote signals or barrier semaphores. Data moves between devices by JAX's collectives and lax.ppermute only.
A program may use at most 128 MiB of HBM per device.

```python
import jax
import jax.numpy as jnp
from jax import lax

D = 8192
FF = 28672
VOCAB = 128256
R = 64
LEN = 32
DOCS = 16
TOKENS = 512
STORED = 4096
EXAMPLES = 1024


def draw_token_ids(key, part):
    len_key = jax.random.fold_in(key, 11)
    tok_key = jax.random.fold_in(key, 12)
    kept_len = jax.random.randint(len_key, (DOCS, 1), LEN // 2, LEN + 1)
    word_ids = jax.random.randint(tok_key, (DOCS, LEN), 1, VOCAB)
    places = jnp.arange(LEN, dtype=jnp.int32)[None, :]
    return jnp.where(places < kept_len, word_ids, 0).reshape(DOCS * LEN).astype(jnp.int32)


def place_ends(values, own_key, least, largest):
    extent = values.shape
    place = [jax.random.randint(jax.random.fold_in(own_key, axis), (), 0, extent[axis]) for axis in range(len(extent))]
    values = values.at[tuple(place)].set(least)
    longest = extent.index(max(extent))
    place[longest] = (place[longest] + 1) % extent[longest]
    return values.at[tuple(place)].set(largest)


def shard_levels(own_key, shape, split, low, top_value):
    level, own = 1.0, jax.random.fold_in(own_key, 6)
    for axis_at, shards_of in split:
        heights = jnp.exp(jax.random.uniform(jax.random.fold_in(own, axis_at), (shards_of,), jnp.float32, low / len(split), top_value / len(split)))
        level = level * jnp.repeat(heights, shape[axis_at] // shards_of).reshape([-1 if axis == axis_at else 1 for axis in range(len(shape))])
    return level


def centred(rng, extent, scale, most, split=(), kind=jnp.bfloat16):
    entries = scale * jax.random.normal(rng, extent, jnp.float32)
    if split:
        entries = entries * shard_levels(rng, extent, split, -0.22, 0.18)
    return jnp.clip(entries, -most, most).astype(kind)


def setup_inputs(seed: int = 0) -> dict:
    streams_of = jax.random.split(jax.random.key(seed), 15)
    return {
        "token_ids": draw_token_ids(jax.random.fold_in(streams_of[14], 71), 0),
        "hidden_in": centred(streams_of[1], (TOKENS, D), 1.0, 6.0, ((0, 16),)),
        "cotangent": centred(streams_of[2], (TOKENS, D), 1.0, 6.0, ((0, 16),)),
        "gate_weight": centred(streams_of[3], (D, FF), D ** -0.5, 0.0625, ((1, 128),)),
        "up_weight": centred(streams_of[4], (D, FF), D ** -0.5, 0.0625, ((1, 128),)),
        "down_weight": centred(streams_of[5], (FF, D), FF ** -0.5, 0.03125, ((0, 128),)),
        "gate_in_proj": centred(streams_of[6], (D, R), D ** -0.5, 0.0625),
        "up_in_proj": centred(streams_of[7], (D, R), D ** -0.5, 0.0625),
        "down_out_proj": centred(streams_of[8], (D, R), D ** -0.5, 0.0625),
        "gate_out_proj": centred(streams_of[9], (FF, R), FF ** -0.5, 0.03125, ((0, 128),)),
        "up_out_proj": centred(streams_of[10], (FF, R), FF ** -0.5, 0.03125, ((0, 128),)),
        "down_in_proj": centred(streams_of[11], (FF, R), FF ** -0.5, 0.03125, ((0, 128),)),
        "stored_grads": centred(streams_of[12], (STORED, 3 * R * R), (3 * R * R) ** -0.5, 0.0546875, ((0, 128),)),
        "example_ids": place_ends(jax.random.randint(streams_of[13], (STORED,), 0, EXAMPLES), jax.random.fold_in(streams_of[13], 1), 0, EXAMPLES - 1).astype(jnp.int32),
    }


def doc_outer(left, right):
    left_docs = left.reshape(DOCS, LEN, R)
    right_docs = right.reshape(DOCS, LEN, R)
    return jnp.einsum("dlr,dls->drs", left_docs, right_docs, precision=lax.Precision.HIGHEST)


def reference(token_ids, hidden_in, cotangent, gate_weight, up_weight, down_weight, gate_in_proj, up_in_proj, down_out_proj, gate_out_proj, up_out_proj, down_in_proj, stored_grads, example_ids):
    pad_mask = (token_ids != 0).astype(jnp.bfloat16)[:, None]
    masked = cotangent * pad_mask
    gate_pre = jnp.dot(hidden_in, gate_weight, preferred_element_type=jnp.float32)
    up_pre = jnp.dot(hidden_in, up_weight, preferred_element_type=jnp.float32)
    squash = jax.nn.sigmoid(gate_pre)
    hidden = (gate_pre * squash * up_pre).astype(jnp.bfloat16)
    back_pre = lax.dot_general(masked, down_weight, (((1,), (1,)), ((), ())), preferred_element_type=jnp.float32)
    grad_up = (back_pre * gate_pre * squash).astype(jnp.bfloat16)
    grad_gate = (back_pre * up_pre * squash * (1.0 + gate_pre * (1.0 - squash))).astype(jnp.bfloat16)
    side_gate = jnp.dot(grad_gate, gate_out_proj, preferred_element_type=jnp.float32)
    side_up = jnp.dot(grad_up, up_out_proj, preferred_element_type=jnp.float32)
    side_down = jnp.dot(hidden, down_in_proj, preferred_element_type=jnp.float32)
    in_gate = jnp.dot(hidden_in, gate_in_proj, preferred_element_type=jnp.float32)
    in_up = jnp.dot(hidden_in, up_in_proj, preferred_element_type=jnp.float32)
    out_down = jnp.dot(masked, down_out_proj, preferred_element_type=jnp.float32)
    blocks = jnp.stack([doc_outer(in_gate, side_gate), doc_outer(in_up, side_up), doc_outer(side_down, out_down)], axis=1)
    doc_grads = blocks.reshape(DOCS, 3 * R * R).astype(jnp.bfloat16)
    scores = lax.dot_general(doc_grads, stored_grads, (((1,), (1,)), ((), ())), preferred_element_type=jnp.float32)
    onehot = (example_ids[:, None] == jnp.arange(EXAMPLES, dtype=jnp.int32)[None, :]).astype(jnp.float32)
    example_scores = jnp.dot(scores, onehot, precision=lax.Precision.HIGHEST)
    return doc_grads, example_scores
```

```python
import jax
import jax.numpy as jnp
from jax import lax
from jax.sharding import PartitionSpec as P

LEN = 32
EX_DEV = 8
ALL = ("dp", "tensor")


def through_layer(act_rows, cot_rows, gate_part, up_part, down_part):
    gate_pre = jnp.dot(act_rows, gate_part, preferred_element_type=jnp.float32)
    up_pre = jnp.dot(act_rows, up_part, preferred_element_type=jnp.float32)
    back_pre = lax.dot_general(
        cot_rows, down_part, (((1,), (1,)), ((), ())), preferred_element_type=jnp.float32
    )
    return (gate_pre, up_pre, back_pre)


def project_rows(gate_pre, up_pre, back_pre, gate_out_proj, up_out_proj, down_in_proj):
    squash = jax.nn.sigmoid(gate_pre)
    hidden = (gate_pre * squash * up_pre).astype(jnp.bfloat16)
    grad_up = (back_pre * gate_pre * squash).astype(jnp.bfloat16)
    grad_gate = (back_pre * up_pre * squash * (1.0 + gate_pre * (1.0 - squash))).astype(
        jnp.bfloat16
    )
    side_gate = jnp.dot(grad_gate, gate_out_proj, preferred_element_type=jnp.float32)
    side_up = jnp.dot(grad_up, up_out_proj, preferred_element_type=jnp.float32)
    side_down = jnp.dot(hidden, down_in_proj, preferred_element_type=jnp.float32)
    return jnp.concatenate([side_gate, side_up, side_down], axis=1)


def scatter_sum(x, n):
    blocks = x.reshape((n, x.shape[0] // n) + x.shape[1:])
    return jnp.sum(lax.all_to_all(blocks, ALL, 0, 0, tiled=False), axis=0)


def gather_rows(x, n):
    copies = jnp.broadcast_to(x[None], (n,) + x.shape)
    got = lax.all_to_all(copies, ALL, 0, 0, tiled=False)
    return got.reshape((n * x.shape[0],) + x.shape[1:])


def body(
    token_ids,
    hidden_in,
    cotangent,
    gate_weight,
    up_weight,
    down_weight,
    gate_in_proj,
    up_in_proj,
    down_out_proj,
    gate_out_proj,
    up_out_proj,
    down_in_proj,
    stored_grads,
    example_ids,
):
    n_all = lax.axis_size("dp") * lax.axis_size("tensor")
    proj_rank = gate_in_proj.shape[1]
    pad_mask = (token_ids != 0).astype(jnp.bfloat16)[:, None]
    masked = cotangent * pad_mask
    act_rows = lax.all_gather(hidden_in, "dp", axis=0, tiled=True)
    cot_rows = lax.all_gather(masked, "dp", axis=0, tiled=True)
    gate_pre, up_pre, back_pre = through_layer(
        act_rows, cot_rows, gate_weight, up_weight, down_weight
    )
    block = project_rows(gate_pre, up_pre, back_pre, gate_out_proj, up_out_proj, down_in_proj)
    summed = gather_rows(scatter_sum(block, n_all), n_all)
    in_gate = jnp.dot(act_rows, gate_in_proj, preferred_element_type=jnp.float32)
    in_up = jnp.dot(act_rows, up_in_proj, preferred_element_type=jnp.float32)
    out_down = jnp.dot(cot_rows, down_out_proj, preferred_element_type=jnp.float32)
    docs = act_rows.shape[0] // LEN

    def doc_outer(left, right):
        left_docs = left.reshape(docs, LEN, proj_rank)
        right_docs = right.reshape(docs, LEN, proj_rank)
        return jnp.einsum("dlr,dls->drs", left_docs, right_docs, precision=lax.Precision.HIGHEST)

    side_gate = summed[:, :proj_rank]
    side_up = summed[:, proj_rank : 2 * proj_rank]
    side_down = summed[:, 2 * proj_rank :]
    blocks = jnp.stack(
        [doc_outer(in_gate, side_gate), doc_outer(in_up, side_up), doc_outer(side_down, out_down)],
        axis=1,
    )
    all_docs = blocks.reshape(docs, 3 * proj_rank * proj_rank).astype(jnp.bfloat16)
    docs_here = hidden_in.shape[0] // LEN
    doc_grads = lax.dynamic_slice_in_dim(all_docs, lax.axis_index("dp") * docs_here, docs_here, 0)
    examples_all = EX_DEV * n_all
    onehot = (example_ids[:, None] == jnp.arange(examples_all, dtype=jnp.int32)[None, :]).astype(
        jnp.float32
    )
    raw_scores = lax.dot_general(
        all_docs,
        stored_grads,
        (((1,), (1,)), ((), ())),
        preferred_element_type=jnp.float32,
    )
    partial_scores = jnp.dot(raw_scores, onehot, precision=lax.Precision.HIGHEST)
    totals = scatter_sum(partial_scores.T, n_all).T
    return (doc_grads, totals)


def solution(mesh):
    return jax.shard_map(
        body,
        mesh=mesh,
        in_specs=(
            P("dp"),
            P("dp", None),
            P("dp", None),
            P(None, ("dp", "tensor")),
            P(None, ("dp", "tensor")),
            P(("dp", "tensor"), None),
            P(),
            P(),
            P(),
            P(("dp", "tensor"), None),
            P(("dp", "tensor"), None),
            P(("dp", "tensor"), None),
            P(("dp", "tensor"), None),
            P(("dp", "tensor")),
        ),
        out_specs=(P("dp", None), P(None, ("dp", "tensor"))),
        check_vma=False,
    )
```

```python
import jax
import jax.numpy as jnp
from jax import lax
from jax.sharding import PartitionSpec as P

LEN = 32
EX_DEV = 8
ALL = ("dp", "tensor")


def through_layer(act_rows, cot_rows, gate_part, up_part, down_part):
    gate_pre = jnp.dot(act_rows, gate_part, preferred_element_type=jnp.float32)
    up_pre = jnp.dot(act_rows, up_part, preferred_element_type=jnp.float32)
    back_pre = lax.dot_general(
        cot_rows, down_part, (((1,), (1,)), ((), ())), preferred_element_type=jnp.float32
    )
    return (gate_pre, up_pre, back_pre)


def project_rows(gate_pre, up_pre, back_pre, gate_out_proj, up_out_proj, down_in_proj):
    squash = jax.nn.sigmoid(gate_pre)
    hidden = (gate_pre * squash * up_pre).astype(jnp.bfloat16)
    grad_up = (back_pre * gate_pre * squash).astype(jnp.bfloat16)
    grad_gate = (back_pre * up_pre * squash * (1.0 + gate_pre * (1.0 - squash))).astype(
        jnp.bfloat16
    )
    side_gate = jnp.dot(grad_gate, gate_out_proj, preferred_element_type=jnp.float32)
    side_up = jnp.dot(grad_up, up_out_proj, preferred_element_type=jnp.float32)
    side_down = jnp.dot(hidden, down_in_proj, preferred_element_type=jnp.float32)
    return jnp.concatenate([side_gate, side_up, side_down], axis=1)


def scatter_sum(x, n):
    blocks = x.reshape((n, x.shape[0] // n) + x.shape[1:])
    return jnp.sum(lax.all_to_all(blocks, ALL, 0, 0, tiled=False), axis=0)


def gather_rows(x, n):
    copies = jnp.broadcast_to(x[None], (n,) + x.shape)
    got = lax.all_to_all(copies, ALL, 0, 0, tiled=False)
    return got.reshape((n * x.shape[0],) + x.shape[1:])


def body(
    token_ids,
    hidden_in,
    cotangent,
    gate_weight,
    up_weight,
    down_weight,
    gate_in_proj,
    up_in_proj,
    down_out_proj,
    gate_out_proj,
    up_out_proj,
    down_in_proj,
    stored_grads,
    example_ids,
):
    n_all = lax.axis_size("dp") * lax.axis_size("tensor")
    proj_rank = gate_in_proj.shape[1]
    pad_mask = (token_ids != 0).astype(jnp.bfloat16)[:, None]
    masked = cotangent * pad_mask
    both = lax.all_gather(jnp.concatenate([hidden_in, masked], axis=1), "dp", axis=0, tiled=True)
    act_rows = both[:, : hidden_in.shape[1]]
    cot_rows = both[:, hidden_in.shape[1] :]
    gate_pre, up_pre, back_pre = through_layer(
        act_rows, cot_rows, gate_weight, up_weight, down_weight
    )
    block = project_rows(gate_pre, up_pre, back_pre, gate_out_proj, up_out_proj, down_in_proj)
    summed = gather_rows(scatter_sum(block, n_all), n_all)
    in_gate = jnp.dot(act_rows, gate_in_proj, preferred_element_type=jnp.float32)
    in_up = jnp.dot(act_rows, up_in_proj, preferred_element_type=jnp.float32)
    out_down = jnp.dot(cot_rows, down_out_proj, preferred_element_type=jnp.float32)
    docs = act_rows.shape[0] // LEN

    def doc_outer(left, right):
        left_docs = left.reshape(docs, LEN, proj_rank)
        right_docs = right.reshape(docs, LEN, proj_rank)
        return jnp.einsum("dlr,dls->drs", left_docs, right_docs, precision=lax.Precision.HIGHEST)

    side_gate = summed[:, :proj_rank]
    side_up = summed[:, proj_rank : 2 * proj_rank]
    side_down = summed[:, 2 * proj_rank :]
    blocks = jnp.stack(
        [doc_outer(in_gate, side_gate), doc_outer(in_up, side_up), doc_outer(side_down, out_down)],
        axis=1,
    )
    all_docs = blocks.reshape(docs, 3 * proj_rank * proj_rank).astype(jnp.bfloat16)
    docs_here = hidden_in.shape[0] // LEN
    doc_grads = lax.dynamic_slice_in_dim(all_docs, lax.axis_index("dp") * docs_here, docs_here, 0)
    examples_all = EX_DEV * n_all
    onehot = (example_ids[:, None] == jnp.arange(examples_all, dtype=jnp.int32)[None, :]).astype(
        jnp.float32
    )
    raw_scores = lax.dot_general(
        all_docs,
        stored_grads,
        (((1,), (1,)), ((), ())),
        preferred_element_type=jnp.float32,
    )
    partial_scores = jnp.dot(raw_scores, onehot, precision=lax.Precision.HIGHEST)
    totals = scatter_sum(partial_scores.T, n_all).T
    return (doc_grads, totals)


def solution(mesh):
    return jax.shard_map(
        body,
        mesh=mesh,
        in_specs=(
            P("dp"),
            P("dp", None),
            P("dp", None),
            P(None, ("dp", "tensor")),
            P(None, ("dp", "tensor")),
            P(("dp", "tensor"), None),
            P(),
            P(),
            P(),
            P(("dp", "tensor"), None),
            P(("dp", "tensor"), None),
            P(("dp", "tensor"), None),
            P(("dp", "tensor"), None),
            P(("dp", "tensor")),
        ),
        out_specs=(P("dp", None), P(None, ("dp", "tensor"))),
        check_vma=False,
    )
```

```python
import jax
import jax.numpy as jnp
from jax import lax
from jax.sharding import PartitionSpec as P

from jax.experimental import pallas as pl
from jax.experimental.pallas import tpu as pltpu

LEN = 32
EX_DEV = 8
ALL = ("dp", "tensor")

KC = 1024


def layer_kernel(act_ref, cot_ref, gw_ref, uw_ref, dw_ref, gi_ref, ui_ref, do_ref,
                 go_ref, uo_ref, di_ref, side_ref, inp_ref, g_acc, u_acc, b_acc, i_acc):
    k = pl.program_id(0)

    @pl.when(k == 0)
    def _():
        g_acc[...] = jnp.zeros_like(g_acc)
        u_acc[...] = jnp.zeros_like(u_acc)
        b_acc[...] = jnp.zeros_like(b_acc)
        i_acc[...] = jnp.zeros_like(i_acc)

    a = act_ref[...]
    c = cot_ref[...]
    f32 = jnp.float32
    g_acc[...] += jnp.dot(a, gw_ref[...], preferred_element_type=f32)
    u_acc[...] += jnp.dot(a, uw_ref[...], preferred_element_type=f32)
    b_acc[...] += lax.dot_general(c, dw_ref[...], (((1,), (1,)), ((), ())), preferred_element_type=f32)
    r = gi_ref.shape[1]
    i_acc[:, 0:r] += jnp.dot(a, gi_ref[...], preferred_element_type=f32)
    i_acc[:, r:2 * r] += jnp.dot(a, ui_ref[...], preferred_element_type=f32)
    i_acc[:, 2 * r:3 * r] += jnp.dot(c, do_ref[...], preferred_element_type=f32)

    @pl.when(k == pl.num_programs(0) - 1)
    def _():
        g = g_acc[...]
        u = u_acc[...]
        b = b_acc[...]
        s = jax.nn.sigmoid(g)
        hidden = (g * s * u).astype(jnp.bfloat16)
        grad_up = (b * g * s).astype(jnp.bfloat16)
        grad_gate = (b * u * s * (1.0 + g * (1.0 - s))).astype(jnp.bfloat16)
        side_ref[:, 0:r] = jnp.dot(grad_gate, go_ref[...], preferred_element_type=f32)
        side_ref[:, r:2 * r] = jnp.dot(grad_up, uo_ref[...], preferred_element_type=f32)
        side_ref[:, 2 * r:3 * r] = jnp.dot(hidden, di_ref[...], preferred_element_type=f32)
        inp_ref[...] = i_acc[...]


def layer_call(both, gw, uw, dw, gi, ui, do, go, uo, di):
    rows, width = both.shape
    d = width // 2
    ff = gw.shape[1]
    r = gi.shape[1]
    nk = d // KC
    f32 = jnp.float32
    full = lambda shape: pl.BlockSpec(shape, lambda k: (0, 0))
    return pl.pallas_call(
        layer_kernel,
        grid=(nk,),
        in_specs=[
            pl.BlockSpec((rows, KC), lambda k: (0, k)),
            pl.BlockSpec((rows, KC), lambda k: (0, k + nk)),
            pl.BlockSpec((KC, ff), lambda k: (k, 0)),
            pl.BlockSpec((KC, ff), lambda k: (k, 0)),
            pl.BlockSpec((ff, KC), lambda k: (0, k)),
            pl.BlockSpec((KC, r), lambda k: (k, 0)),
            pl.BlockSpec((KC, r), lambda k: (k, 0)),
            pl.BlockSpec((KC, r), lambda k: (k, 0)),
            full((ff, r)),
            full((ff, r)),
            full((ff, r)),
        ],
        out_specs=[full((rows, 3 * r)), full((rows, 3 * r))],
        out_shape=[jax.ShapeDtypeStruct((rows, 3 * r), f32), jax.ShapeDtypeStruct((rows, 3 * r), f32)],
        scratch_shapes=[
            pltpu.VMEM((rows, ff), f32),
            pltpu.VMEM((rows, ff), f32),
            pltpu.VMEM((rows, ff), f32),
            pltpu.VMEM((rows, 3 * r), f32),
        ],
        compiler_params=pltpu.CompilerParams(dimension_semantics=("arbitrary",)),
        cost_estimate=pl.CostEstimate(
            flops=2 * rows * d * (3 * ff + 3 * r) + 2 * rows * ff * 3 * r,
            transcendentals=rows * ff,
            bytes_accessed=2 * (rows * width + 3 * d * ff + 3 * d * r + 3 * ff * r) + 8 * rows * 3 * r,
        ),
    )(both, both, gw, uw, dw, gi, ui, do, go, uo, di)


def scatter_sum(x, n):
    blocks = x.reshape((n, x.shape[0] // n) + x.shape[1:])
    return jnp.sum(lax.all_to_all(blocks, ALL, 0, 0, tiled=False), axis=0)


def gather_rows(x, n):
    copies = jnp.broadcast_to(x[None], (n,) + x.shape)
    got = lax.all_to_all(copies, ALL, 0, 0, tiled=False)
    return got.reshape((n * x.shape[0],) + x.shape[1:])


def body(
    token_ids,
    hidden_in,
    cotangent,
    gate_weight,
    up_weight,
    down_weight,
    gate_in_proj,
    up_in_proj,
    down_out_proj,
    gate_out_proj,
    up_out_proj,
    down_in_proj,
    stored_grads,
    example_ids,
):
    n_all = lax.axis_size("dp") * lax.axis_size("tensor")
    proj_rank = gate_in_proj.shape[1]
    pad_mask = (token_ids != 0).astype(jnp.bfloat16)[:, None]
    masked = cotangent * pad_mask
    both = lax.all_gather(jnp.concatenate([hidden_in, masked], axis=1), "dp", axis=0, tiled=True)
    block, inputs = layer_call(
        both, gate_weight, up_weight, down_weight, gate_in_proj, up_in_proj, down_out_proj,
        gate_out_proj, up_out_proj, down_in_proj,
    )
    summed = gather_rows(scatter_sum(block, n_all), n_all)
    in_gate = inputs[:, :proj_rank]
    in_up = inputs[:, proj_rank : 2 * proj_rank]
    out_down = inputs[:, 2 * proj_rank :]
    docs = both.shape[0] // LEN

    def doc_outer(left, right):
        left_docs = left.reshape(docs, LEN, proj_rank)
        right_docs = right.reshape(docs, LEN, proj_rank)
        return jnp.einsum("dlr,dls->drs", left_docs, right_docs, precision=lax.Precision.HIGHEST)

    side_gate = summed[:, :proj_rank]
    side_up = summed[:, proj_rank : 2 * proj_rank]
    side_down = summed[:, 2 * proj_rank :]
    blocks = jnp.stack(
        [doc_outer(in_gate, side_gate), doc_outer(in_up, side_up), doc_outer(side_down, out_down)],
        axis=1,
    )
    all_docs = blocks.reshape(docs, 3 * proj_rank * proj_rank).astype(jnp.bfloat16)
    docs_here = hidden_in.shape[0] // LEN
    doc_grads = lax.dynamic_slice_in_dim(all_docs, lax.axis_index("dp") * docs_here, docs_here, 0)
    examples_all = EX_DEV * n_all
    onehot = (example_ids[:, None] == jnp.arange(examples_all, dtype=jnp.int32)[None, :]).astype(
        jnp.float32
    )
    raw_scores = lax.dot_general(
        all_docs,
        stored_grads,
        (((1,), (1,)), ((), ())),
        preferred_element_type=jnp.float32,
    )
    partial_scores = jnp.dot(raw_scores, onehot, precision=lax.Precision.HIGHEST)
    totals = scatter_sum(partial_scores.T, n_all).T
    return (doc_grads, totals)


def solution(mesh):
    return jax.shard_map(
        body,
        mesh=mesh,
        in_specs=(
            P("dp"),
            P("dp", None),
            P("dp", None),
            P(None, ("dp", "tensor")),
            P(None, ("dp", "tensor")),
            P(("dp", "tensor"), None),
            P(),
            P(),
            P(),
            P(("dp", "tensor"), None),
            P(("dp", "tensor"), None),
            P(("dp", "tensor"), None),
            P(("dp", "tensor"), None),
            P(("dp", "tensor")),
        ),
        out_specs=(P("dp", None), P(None, ("dp", "tensor"))),
        check_vma=False,
    )
```

```python
import jax
import jax.numpy as jnp
from jax import lax
from jax.sharding import PartitionSpec as P

from jax.experimental import pallas as pl
from jax.experimental.pallas import tpu as pltpu

LEN = 32
EX_DEV = 8
ALL = ("dp", "tensor")

KC = 2048
LANE = 128


def pad_to(x, cols):
    return jnp.pad(x, ((0, 0), (0, cols - x.shape[1])))


def layer_kernel(act_ref, cot_ref, wa_ref, wc_ref, go_ref, uo_ref, di_ref, side_ref, inp_ref, a_acc, c_acc):
    k = pl.program_id(0)

    @pl.when(k == 0)
    def _():
        a_acc[...] = jnp.zeros_like(a_acc)
        c_acc[...] = jnp.zeros_like(c_acc)

    f32 = jnp.float32
    a_acc[...] += jnp.dot(act_ref[...], wa_ref[...], preferred_element_type=f32)
    c_acc[...] += jnp.dot(cot_ref[...], wc_ref[...], preferred_element_type=f32)

    @pl.when(k == pl.num_programs(0) - 1)
    def _():
        ff, r = go_ref.shape
        fp = -(-ff // LANE) * LANE
        g = a_acc[:, 0:ff]
        u = a_acc[:, fp : fp + ff]
        b = c_acc[:, 0:ff]
        s = jax.nn.sigmoid(g)
        hidden = (g * s * u).astype(jnp.bfloat16)
        grad_up = (b * g * s).astype(jnp.bfloat16)
        grad_gate = (b * u * s * (1.0 + g * (1.0 - s))).astype(jnp.bfloat16)
        side_ref[:, 0:r] = jnp.dot(grad_gate, go_ref[...], preferred_element_type=f32)
        side_ref[:, r : 2 * r] = jnp.dot(grad_up, uo_ref[...], preferred_element_type=f32)
        side_ref[:, 2 * r : 3 * r] = jnp.dot(hidden, di_ref[...], preferred_element_type=f32)
        inp_ref[:, 0 : 2 * r] = a_acc[:, 2 * fp : 2 * fp + 2 * r]
        inp_ref[:, 2 * r : 3 * r] = c_acc[:, fp : fp + r]


def layer_call(both, gw, uw, dw, gi, ui, do, go, uo, di):
    rows, width = both.shape
    d = width // 2
    ff = gw.shape[1]
    r = gi.shape[1]
    fp = -(-ff // LANE) * LANE
    wa = jnp.concatenate([pad_to(gw, fp), pad_to(uw, fp), pad_to(jnp.concatenate([gi, ui], 1), LANE)], 1)
    wc = jnp.concatenate([pad_to(dw.T, fp), pad_to(do, LANE)], 1)
    nk = d // KC
    f32 = jnp.float32
    full = lambda shape: pl.BlockSpec(shape, lambda k: (0, 0))
    return pl.pallas_call(
        layer_kernel,
        grid=(nk,),
        in_specs=[
            pl.BlockSpec((rows, KC), lambda k: (0, k)),
            pl.BlockSpec((rows, KC), lambda k: (0, k + nk)),
            pl.BlockSpec((KC, wa.shape[1]), lambda k: (k, 0)),
            pl.BlockSpec((KC, wc.shape[1]), lambda k: (k, 0)),
            full((ff, r)),
            full((ff, r)),
            full((ff, r)),
        ],
        out_specs=[full((rows, 3 * r)), full((rows, 3 * r))],
        out_shape=[jax.ShapeDtypeStruct((rows, 3 * r), f32), jax.ShapeDtypeStruct((rows, 3 * r), f32)],
        scratch_shapes=[
            pltpu.VMEM((rows, wa.shape[1]), f32),
            pltpu.VMEM((rows, wc.shape[1]), f32),
        ],
        compiler_params=pltpu.CompilerParams(
            dimension_semantics=("arbitrary",), vmem_limit_bytes=48 * 1024 * 1024
        ),
        cost_estimate=pl.CostEstimate(
            flops=2 * rows * d * (3 * ff + 3 * r) + 2 * rows * ff * 3 * r,
            transcendentals=rows * ff,
            bytes_accessed=2 * (rows * width + d * (wa.shape[1] + wc.shape[1]) + 3 * ff * r) + 8 * rows * 3 * r,
        ),
    )(both, both, wa, wc, go, uo, di)


def scatter_sum(x, n):
    blocks = x.reshape((n, x.shape[0] // n) + x.shape[1:])
    return jnp.sum(lax.all_to_all(blocks, ALL, 0, 0, tiled=False), axis=0)


def gather_rows(x, n):
    copies = jnp.broadcast_to(x[None], (n,) + x.shape)
    got = lax.all_to_all(copies, ALL, 0, 0, tiled=False)
    return got.reshape((n * x.shape[0],) + x.shape[1:])


def body(
    token_ids,
    hidden_in,
    cotangent,
    gate_weight,
    up_weight,
    down_weight,
    gate_in_proj,
    up_in_proj,
    down_out_proj,
    gate_out_proj,
    up_out_proj,
    down_in_proj,
    stored_grads,
    example_ids,
):
    n_all = lax.axis_size("dp") * lax.axis_size("tensor")
    proj_rank = gate_in_proj.shape[1]
    pad_mask = (token_ids != 0).astype(jnp.bfloat16)[:, None]
    masked = cotangent * pad_mask
    both = lax.all_gather(jnp.concatenate([hidden_in, masked], axis=1), "dp", axis=0, tiled=True)
    block, inputs = layer_call(
        both, gate_weight, up_weight, down_weight, gate_in_proj, up_in_proj, down_out_proj,
        gate_out_proj, up_out_proj, down_in_proj,
    )
    summed = gather_rows(scatter_sum(block, n_all), n_all)
    in_gate = inputs[:, :proj_rank]
    in_up = inputs[:, proj_rank : 2 * proj_rank]
    out_down = inputs[:, 2 * proj_rank :]
    docs = both.shape[0] // LEN

    def doc_outer(left, right):
        left_docs = left.reshape(docs, LEN, proj_rank)
        right_docs = right.reshape(docs, LEN, proj_rank)
        return jnp.einsum("dlr,dls->drs", left_docs, right_docs, precision=lax.Precision.HIGHEST)

    side_gate = summed[:, :proj_rank]
    side_up = summed[:, proj_rank : 2 * proj_rank]
    side_down = summed[:, 2 * proj_rank :]
    blocks = jnp.stack(
        [doc_outer(in_gate, side_gate), doc_outer(in_up, side_up), doc_outer(side_down, out_down)],
        axis=1,
    )
    all_docs = blocks.reshape(docs, 3 * proj_rank * proj_rank).astype(jnp.bfloat16)
    docs_here = hidden_in.shape[0] // LEN
    doc_grads = lax.dynamic_slice_in_dim(all_docs, lax.axis_index("dp") * docs_here, docs_here, 0)
    examples_all = EX_DEV * n_all
    onehot = (example_ids[:, None] == jnp.arange(examples_all, dtype=jnp.int32)[None, :]).astype(
        jnp.float32
    )
    raw_scores = lax.dot_general(
        all_docs,
        stored_grads,
        (((1,), (1,)), ((), ())),
        preferred_element_type=jnp.float32,
    )
    partial_scores = jnp.dot(raw_scores, onehot, precision=lax.Precision.HIGHEST)
    totals = scatter_sum(partial_scores.T, n_all).T
    return (doc_grads, totals)


def solution(mesh):
    return jax.shard_map(
        body,
        mesh=mesh,
        in_specs=(
            P("dp"),
            P("dp", None),
            P("dp", None),
            P(None, ("dp", "tensor")),
            P(None, ("dp", "tensor")),
            P(("dp", "tensor"), None),
            P(),
            P(),
            P(),
            P(("dp", "tensor"), None),
            P(("dp", "tensor"), None),
            P(("dp", "tensor"), None),
            P(("dp", "tensor"), None),
            P(("dp", "tensor")),
        ),
        out_specs=(P("dp", None), P(None, ("dp", "tensor"))),
        check_vma=False,
    )
```

```python
import jax
import jax.numpy as jnp
from jax import lax
from jax.sharding import PartitionSpec as P

from jax.experimental import pallas as pl
from jax.experimental.pallas import tpu as pltpu

LEN = 32
EX_DEV = 8
ALL = ("dp", "tensor")

KC = 2048
LANE = 128


def pad_to(x, cols):
    return jnp.pad(x, ((0, 0), (0, cols - x.shape[1])))


def layer_kernel(act_ref, cot_ref, wa_ref, wc_ref, go_ref, uo_ref, di_ref, side_ref, a_acc, c_acc):
    k = pl.program_id(0)

    @pl.when(k == 0)
    def _():
        a_acc[...] = jnp.zeros_like(a_acc)
        c_acc[...] = jnp.zeros_like(c_acc)

    f32 = jnp.float32
    a_acc[...] += jnp.dot(act_ref[...], wa_ref[...], preferred_element_type=f32)
    c_acc[...] += jnp.dot(cot_ref[...], wc_ref[...], preferred_element_type=f32)

    @pl.when(k == pl.num_programs(0) - 1)
    def _():
        ff, r = go_ref.shape
        fp = -(-ff // LANE) * LANE
        g = a_acc[:, 0:ff]
        u = a_acc[:, fp : fp + ff]
        b = c_acc[:, 0:ff]
        s = jax.nn.sigmoid(g)
        hidden = (g * s * u).astype(jnp.bfloat16)
        grad_up = (b * g * s).astype(jnp.bfloat16)
        grad_gate = (b * u * s * (1.0 + g * (1.0 - s))).astype(jnp.bfloat16)
        side_ref[:, 0:r] = jnp.dot(grad_gate, go_ref[...], preferred_element_type=f32)
        side_ref[:, r : 2 * r] = jnp.dot(grad_up, uo_ref[...], preferred_element_type=f32)
        side_ref[:, 2 * r : 3 * r] = jnp.dot(hidden, di_ref[...], preferred_element_type=f32)


def layer_call(both, gw, uw, dw, go, uo, di):
    rows, width = both.shape
    d = width // 2
    ff = gw.shape[1]
    r = go.shape[1]
    fp = -(-ff // LANE) * LANE
    wa = jnp.concatenate([pad_to(gw, fp), pad_to(uw, fp)], 1)
    wc = pad_to(dw.T, fp)
    nk = d // KC
    f32 = jnp.float32
    full = lambda shape: pl.BlockSpec(shape, lambda k: (0, 0))
    return pl.pallas_call(
        layer_kernel,
        grid=(nk,),
        in_specs=[
            pl.BlockSpec((rows, KC), lambda k: (0, k)),
            pl.BlockSpec((rows, KC), lambda k: (0, k + nk)),
            pl.BlockSpec((KC, wa.shape[1]), lambda k: (k, 0)),
            pl.BlockSpec((KC, wc.shape[1]), lambda k: (k, 0)),
            full((ff, r)),
            full((ff, r)),
            full((ff, r)),
        ],
        out_specs=full((rows, 3 * r)),
        out_shape=jax.ShapeDtypeStruct((rows, 3 * r), f32),
        scratch_shapes=[
            pltpu.VMEM((rows, wa.shape[1]), f32),
            pltpu.VMEM((rows, wc.shape[1]), f32),
        ],
        compiler_params=pltpu.CompilerParams(
            dimension_semantics=("arbitrary",), vmem_limit_bytes=48 * 1024 * 1024
        ),
        cost_estimate=pl.CostEstimate(
            flops=2 * rows * d * 3 * ff + 2 * rows * ff * 3 * r,
            transcendentals=rows * ff,
            bytes_accessed=2 * (rows * width + d * (wa.shape[1] + wc.shape[1]) + 3 * ff * r) + 4 * rows * 3 * r,
        ),
    )(both, both, wa, wc, go, uo, di)


def scatter_sum(x, n):
    blocks = x.reshape((n, x.shape[0] // n) + x.shape[1:])
    return jnp.sum(lax.all_to_all(blocks, ALL, 0, 0, tiled=False), axis=0)


def gather_rows(x, n):
    copies = jnp.broadcast_to(x[None], (n,) + x.shape)
    got = lax.all_to_all(copies, ALL, 0, 0, tiled=False)
    return got.reshape((n * x.shape[0],) + x.shape[1:])


def body(
    token_ids,
    hidden_in,
    cotangent,
    gate_weight,
    up_weight,
    down_weight,
    gate_in_proj,
    up_in_proj,
    down_out_proj,
    gate_out_proj,
    up_out_proj,
    down_in_proj,
    stored_grads,
    example_ids,
):
    n_all = lax.axis_size("dp") * lax.axis_size("tensor")
    proj_rank = gate_in_proj.shape[1]
    pad_mask = (token_ids != 0).astype(jnp.bfloat16)[:, None]
    masked = cotangent * pad_mask
    both = lax.all_gather(jnp.concatenate([hidden_in, masked], axis=1), "dp", axis=0, tiled=True)
    f32 = jnp.float32
    own_inputs = jnp.concatenate(
        [
            jnp.dot(hidden_in, gate_in_proj, preferred_element_type=f32),
            jnp.dot(hidden_in, up_in_proj, preferred_element_type=f32),
            jnp.dot(masked, down_out_proj, preferred_element_type=f32),
        ],
        axis=1,
    )
    block = layer_call(both, gate_weight, up_weight, down_weight, gate_out_proj, up_out_proj, down_in_proj)
    part_rows = block.shape[0] // n_all
    my_inputs = lax.dynamic_slice_in_dim(own_inputs, lax.axis_index("tensor") * part_rows, part_rows, 0)
    summed_part = scatter_sum(block, n_all)
    gathered = gather_rows(jnp.concatenate([summed_part, my_inputs], axis=1), n_all)
    width = 3 * proj_rank
    summed = gathered[:, :width]
    in_gate = gathered[:, width : width + proj_rank]
    in_up = gathered[:, width + proj_rank : width + 2 * proj_rank]
    out_down = gathered[:, width + 2 * proj_rank :]
    docs = both.shape[0] // LEN

    def doc_outer(left, right):
        left_docs = left.reshape(docs, LEN, proj_rank)
        right_docs = right.reshape(docs, LEN, proj_rank)
        return jnp.einsum("dlr,dls->drs", left_docs, right_docs, precision=lax.Precision.HIGHEST)

    side_gate = summed[:, :proj_rank]
    side_up = summed[:, proj_rank : 2 * proj_rank]
    side_down = summed[:, 2 * proj_rank :]
    blocks = jnp.stack(
        [doc_outer(in_gate, side_gate), doc_outer(in_up, side_up), doc_outer(side_down, out_down)],
        axis=1,
    )
    all_docs = blocks.reshape(docs, 3 * proj_rank * proj_rank).astype(jnp.bfloat16)
    docs_here = hidden_in.shape[0] // LEN
    doc_grads = lax.dynamic_slice_in_dim(all_docs, lax.axis_index("dp") * docs_here, docs_here, 0)
    examples_all = EX_DEV * n_all
    onehot = (example_ids[:, None] == jnp.arange(examples_all, dtype=jnp.int32)[None, :]).astype(
        jnp.float32
    )
    raw_scores = lax.dot_general(
        all_docs,
        stored_grads,
        (((1,), (1,)), ((), ())),
        preferred_element_type=jnp.float32,
    )
    partial_scores = jnp.dot(raw_scores, onehot, precision=lax.Precision.HIGHEST)
    totals = scatter_sum(partial_scores.T, n_all).T
    return (doc_grads, totals)


def solution(mesh):
    return jax.shard_map(
        body,
        mesh=mesh,
        in_specs=(
            P("dp"),
            P("dp", None),
            P("dp", None),
            P(None, ("dp", "tensor")),
            P(None, ("dp", "tensor")),
            P(("dp", "tensor"), None),
            P(),
            P(),
            P(),
            P(("dp", "tensor"), None),
            P(("dp", "tensor"), None),
            P(("dp", "tensor"), None),
            P(("dp", "tensor"), None),
            P(("dp", "tensor")),
        ),
        out_specs=(P("dp", None), P(None, ("dp", "tensor"))),
        check_vma=False,
    )
```

```python
import jax
import jax.numpy as jnp
from jax import lax
from jax.sharding import PartitionSpec as P

from jax.experimental import pallas as pl
from jax.experimental.pallas import tpu as pltpu

LEN = 32
EX_DEV = 8
ALL = ("dp", "tensor")

KC = 2048
LANE = 128


def pad_to(x, cols):
    return jnp.pad(x, ((0, 0), (0, cols - x.shape[1])))


def layer_kernel(act_ref, cot_ref, wa_ref, wc_ref, go_ref, uo_ref, di_ref, side_ref, a_acc, c_acc):
    k = pl.program_id(0)

    @pl.when(k == 0)
    def _():
        a_acc[...] = jnp.zeros_like(a_acc)
        c_acc[...] = jnp.zeros_like(c_acc)

    f32 = jnp.float32
    a_acc[...] += jnp.dot(act_ref[...], wa_ref[...], preferred_element_type=f32)
    c_acc[...] += jnp.dot(cot_ref[...], wc_ref[...], preferred_element_type=f32)

    @pl.when(k == pl.num_programs(0) - 1)
    def _():
        ff, r = go_ref.shape
        fp = -(-ff // LANE) * LANE
        g = a_acc[:, 0:ff]
        u = a_acc[:, fp : fp + ff]
        b = c_acc[:, 0:ff]
        s = jax.nn.sigmoid(g)
        hidden = (g * s * u).astype(jnp.bfloat16)
        grad_up = (b * g * s).astype(jnp.bfloat16)
        grad_gate = (b * u * s * (1.0 + g * (1.0 - s))).astype(jnp.bfloat16)
        side_ref[:, 0:r] = jnp.dot(grad_gate, go_ref[...], preferred_element_type=f32)
        side_ref[:, r : 2 * r] = jnp.dot(grad_up, uo_ref[...], preferred_element_type=f32)
        side_ref[:, 2 * r : 3 * r] = jnp.dot(hidden, di_ref[...], preferred_element_type=f32)


def layer_call(both, gw, uw, dw, go, uo, di):
    rows, width = both.shape
    d = width // 2
    ff = gw.shape[1]
    r = go.shape[1]
    fp = -(-ff // LANE) * LANE
    wa = jnp.concatenate([pad_to(gw, fp), pad_to(uw, fp)], 1)
    wc = pad_to(dw.T, fp)
    nk = d // KC
    f32 = jnp.float32
    full = lambda shape: pl.BlockSpec(shape, lambda k: (0, 0))
    return pl.pallas_call(
        layer_kernel,
        grid=(nk,),
        in_specs=[
            pl.BlockSpec((rows, KC), lambda k: (0, k)),
            pl.BlockSpec((rows, KC), lambda k: (0, k + nk)),
            pl.BlockSpec((KC, wa.shape[1]), lambda k: (k, 0)),
            pl.BlockSpec((KC, wc.shape[1]), lambda k: (k, 0)),
            full((ff, r)),
            full((ff, r)),
            full((ff, r)),
        ],
        out_specs=full((rows, 3 * r)),
        out_shape=jax.ShapeDtypeStruct((rows, 3 * r), f32),
        scratch_shapes=[
            pltpu.VMEM((rows, wa.shape[1]), f32),
            pltpu.VMEM((rows, wc.shape[1]), f32),
        ],
        compiler_params=pltpu.CompilerParams(
            dimension_semantics=("arbitrary",), vmem_limit_bytes=62 * 1024 * 1024
        ),
        cost_estimate=pl.CostEstimate(
            flops=2 * rows * d * 3 * ff + 2 * rows * ff * 3 * r,
            transcendentals=rows * ff,
            bytes_accessed=2 * (rows * width + d * (wa.shape[1] + wc.shape[1]) + 3 * ff * r) + 4 * rows * 3 * r,
        ),
    )(both, both, wa, wc, go, uo, di)


def scatter_sum(x, n):
    blocks = x.reshape((n, x.shape[0] // n) + x.shape[1:])
    return jnp.sum(lax.all_to_all(blocks, ALL, 0, 0, tiled=False), axis=0)


def gather_rows(x, n):
    copies = jnp.broadcast_to(x[None], (n,) + x.shape)
    got = lax.all_to_all(copies, ALL, 0, 0, tiled=False)
    return got.reshape((n * x.shape[0],) + x.shape[1:])


def body(
    token_ids,
    hidden_in,
    cotangent,
    gate_weight,
    up_weight,
    down_weight,
    gate_in_proj,
    up_in_proj,
    down_out_proj,
    gate_out_proj,
    up_out_proj,
    down_in_proj,
    stored_grads,
    example_ids,
):
    n_all = lax.axis_size("dp") * lax.axis_size("tensor")
    proj_rank = gate_in_proj.shape[1]
    pad_mask = (token_ids != 0).astype(jnp.bfloat16)[:, None]
    masked = cotangent * pad_mask
    both = lax.all_gather(jnp.concatenate([hidden_in, masked], axis=1), "dp", axis=0, tiled=True)
    f32 = jnp.float32
    block = layer_call(both, gate_weight, up_weight, down_weight, gate_out_proj, up_out_proj, down_in_proj)
    summed = gather_rows(scatter_sum(block, n_all), n_all)
    d_model = hidden_in.shape[1]
    in_both = jnp.dot(
        both[:, :d_model], jnp.concatenate([gate_in_proj, up_in_proj], axis=1), preferred_element_type=f32
    )
    in_gate = in_both[:, :proj_rank]
    in_up = in_both[:, proj_rank:]
    out_down = jnp.dot(both[:, d_model:], down_out_proj, preferred_element_type=f32)
    docs = both.shape[0] // LEN

    def doc_outer(left, right):
        left_docs = left.reshape(docs, LEN, proj_rank)
        right_docs = right.reshape(docs, LEN, proj_rank)
        return jnp.einsum("dlr,dls->drs", left_docs, right_docs, precision=lax.Precision.HIGHEST)

    side_gate = summed[:, :proj_rank]
    side_up = summed[:, proj_rank : 2 * proj_rank]
    side_down = summed[:, 2 * proj_rank :]
    blocks = jnp.stack(
        [doc_outer(in_gate, side_gate), doc_outer(in_up, side_up), doc_outer(side_down, out_down)],
        axis=1,
    )
    all_docs = blocks.reshape(docs, 3 * proj_rank * proj_rank).astype(jnp.bfloat16)
    docs_here = hidden_in.shape[0] // LEN
    doc_grads = lax.dynamic_slice_in_dim(all_docs, lax.axis_index("dp") * docs_here, docs_here, 0)
    examples_all = EX_DEV * n_all
    onehot = (example_ids[:, None] == jnp.arange(examples_all, dtype=jnp.int32)[None, :]).astype(
        jnp.float32
    )
    raw_scores = lax.dot_general(
        all_docs,
        stored_grads,
        (((1,), (1,)), ((), ())),
        preferred_element_type=jnp.float32,
    )
    partial_scores = jnp.dot(raw_scores, onehot, precision=lax.Precision.HIGHEST)
    totals = scatter_sum(partial_scores.T, n_all).T
    return (doc_grads, totals)


def solution(mesh):
    return jax.shard_map(
        body,
        mesh=mesh,
        in_specs=(
            P("dp"),
            P("dp", None),
            P("dp", None),
            P(None, ("dp", "tensor")),
            P(None, ("dp", "tensor")),
            P(("dp", "tensor"), None),
            P(),
            P(),
            P(),
            P(("dp", "tensor"), None),
            P(("dp", "tensor"), None),
            P(("dp", "tensor"), None),
            P(("dp", "tensor"), None),
            P(("dp", "tensor")),
        ),
        out_specs=(P("dp", None), P(None, ("dp", "tensor"))),
        check_vma=False,
    )
```

```python
import jax
import jax.numpy as jnp
from jax import lax
from jax.sharding import PartitionSpec as P

from jax.experimental import pallas as pl
from jax.experimental.pallas import tpu as pltpu

LEN = 32
EX_DEV = 8
ALL = ("dp", "tensor")

KC = 2048
LANE = 128


def pad_to(x, cols):
    return jnp.pad(x, ((0, 0), (0, cols - x.shape[1])))


def layer_kernel(act_ref, cot_ref, wa_ref, wc_ref, go_ref, uo_ref, di_ref, side_ref, a_acc, c_acc):
    k = pl.program_id(0)

    @pl.when(k == 0)
    def _():
        a_acc[...] = jnp.zeros_like(a_acc)
        c_acc[...] = jnp.zeros_like(c_acc)

    f32 = jnp.float32
    a_acc[...] += jnp.dot(act_ref[...], wa_ref[...], preferred_element_type=f32)
    c_acc[...] += jnp.dot(cot_ref[...], wc_ref[...], preferred_element_type=f32)

    @pl.when(k == pl.num_programs(0) - 1)
    def _():
        ff, r = go_ref.shape
        fp = -(-ff // LANE) * LANE
        g = a_acc[:, 0:ff]
        u = a_acc[:, fp : fp + ff]
        b = c_acc[:, 0:ff]
        s = jax.nn.sigmoid(g)
        hidden = (g * s * u).astype(jnp.bfloat16)
        grad_up = (b * g * s).astype(jnp.bfloat16)
        grad_gate = (b * u * s * (1.0 + g * (1.0 - s))).astype(jnp.bfloat16)
        side_ref[:, 0:r] = jnp.dot(grad_gate, go_ref[...], preferred_element_type=f32)
        side_ref[:, r : 2 * r] = jnp.dot(grad_up, uo_ref[...], preferred_element_type=f32)
        side_ref[:, 2 * r : 3 * r] = jnp.dot(hidden, di_ref[...], preferred_element_type=f32)


def layer_call(both, gw, uw, dw, go, uo, di):
    rows, width = both.shape
    d = width // 2
    ff = gw.shape[1]
    r = go.shape[1]
    fp = -(-ff // LANE) * LANE
    wa = jnp.concatenate([pad_to(gw, fp), pad_to(uw, fp)], 1)
    wc = pad_to(dw.T, fp)
    nk = d // KC
    f32 = jnp.float32
    full = lambda shape: pl.BlockSpec(shape, lambda k: (0, 0))
    return pl.pallas_call(
        layer_kernel,
        grid=(nk,),
        in_specs=[
            pl.BlockSpec((rows, KC), lambda k: (0, k)),
            pl.BlockSpec((rows, KC), lambda k: (0, k + nk)),
            pl.BlockSpec((KC, wa.shape[1]), lambda k: (k, 0)),
            pl.BlockSpec((KC, wc.shape[1]), lambda k: (k, 0)),
            full((ff, r)),
            full((ff, r)),
            full((ff, r)),
        ],
        out_specs=full((rows, 3 * r)),
        out_shape=jax.ShapeDtypeStruct((rows, 3 * r), f32),
        scratch_shapes=[
            pltpu.VMEM((rows, wa.shape[1]), f32),
            pltpu.VMEM((rows, wc.shape[1]), f32),
        ],
        compiler_params=pltpu.CompilerParams(
            dimension_semantics=("arbitrary",), vmem_limit_bytes=62 * 1024 * 1024
        ),
        cost_estimate=pl.CostEstimate(
            flops=2 * rows * d * 3 * ff + 2 * rows * ff * 3 * r,
            transcendentals=rows * ff,
            bytes_accessed=2 * (rows * width + d * (wa.shape[1] + wc.shape[1]) + 3 * ff * r) + 4 * rows * 3 * r,
        ),
    )(both, both, wa, wc, go, uo, di)


def scatter_sum(x, n):
    blocks = x.reshape((n, x.shape[0] // n) + x.shape[1:])
    return jnp.sum(lax.all_to_all(blocks, ALL, 0, 0, tiled=False), axis=0)


def gather_rows(x, n):
    copies = jnp.broadcast_to(x[None], (n,) + x.shape)
    got = lax.all_to_all(copies, ALL, 0, 0, tiled=False)
    return got.reshape((n * x.shape[0],) + x.shape[1:])


def body(
    token_ids,
    hidden_in,
    cotangent,
    gate_weight,
    up_weight,
    down_weight,
    gate_in_proj,
    up_in_proj,
    down_out_proj,
    gate_out_proj,
    up_out_proj,
    down_in_proj,
    stored_grads,
    example_ids,
):
    n_all = lax.axis_size("dp") * lax.axis_size("tensor")
    proj_rank = gate_in_proj.shape[1]
    pad_mask = (token_ids != 0).astype(jnp.bfloat16)[:, None]
    masked = cotangent * pad_mask
    both = lax.all_gather(jnp.concatenate([hidden_in, masked], axis=1), "dp", axis=0, tiled=True)
    f32 = jnp.float32
    block = layer_call(both, gate_weight, up_weight, down_weight, gate_out_proj, up_out_proj, down_in_proj)
    summed = gather_rows(scatter_sum(block, n_all), n_all)
    d_model = hidden_in.shape[1]
    in_both = jnp.dot(
        both[:, :d_model], jnp.concatenate([gate_in_proj, up_in_proj], axis=1), preferred_element_type=f32
    )
    in_gate = in_both[:, :proj_rank]
    in_up = in_both[:, proj_rank:]
    out_down = jnp.dot(both[:, d_model:], down_out_proj, preferred_element_type=f32)
    docs = both.shape[0] // LEN

    side_gate = summed[:, :proj_rank]
    side_up = summed[:, proj_rank : 2 * proj_rank]
    side_down = summed[:, 2 * proj_rank :]
    shape = (3, docs, LEN, proj_rank)
    lefts = jnp.stack([in_gate, in_up, side_down]).reshape(shape)
    rights = jnp.stack([side_gate, side_up, out_down]).reshape(shape)
    blocks = jnp.einsum("bdlr,bdls->dbrs", lefts, rights, precision=lax.Precision.HIGHEST)
    all_docs = blocks.reshape(docs, 3 * proj_rank * proj_rank).astype(jnp.bfloat16)
    docs_here = hidden_in.shape[0] // LEN
    doc_grads = lax.dynamic_slice_in_dim(all_docs, lax.axis_index("dp") * docs_here, docs_here, 0)
    examples_all = EX_DEV * n_all
    onehot = (example_ids[:, None] == jnp.arange(examples_all, dtype=jnp.int32)[None, :]).astype(
        jnp.float32
    )
    raw_scores = lax.dot_general(
        all_docs,
        stored_grads,
        (((1,), (1,)), ((), ())),
        preferred_element_type=jnp.float32,
    )
    partial_scores = jnp.dot(raw_scores, onehot, precision=lax.Precision.HIGHEST)
    totals = scatter_sum(partial_scores.T, n_all).T
    return (doc_grads, totals)


def solution(mesh):
    return jax.shard_map(
        body,
        mesh=mesh,
        in_specs=(
            P("dp"),
            P("dp", None),
            P("dp", None),
            P(None, ("dp", "tensor")),
            P(None, ("dp", "tensor")),
            P(("dp", "tensor"), None),
            P(),
            P(),
            P(),
            P(("dp", "tensor"), None),
            P(("dp", "tensor"), None),
            P(("dp", "tensor"), None),
            P(("dp", "tensor"), None),
            P(("dp", "tensor")),
        ),
        out_specs=(P("dp", None), P(None, ("dp", "tensor"))),
        check_vma=False,
    )
```

```python
import jax
import jax.numpy as jnp
from jax import lax
from jax.sharding import PartitionSpec as P

from jax.experimental import pallas as pl
from jax.experimental.pallas import tpu as pltpu

LEN = 32
EX_DEV = 8
ALL = ("dp", "tensor")

KC = 1024
LANE = 128


def pad_to(x, cols):
    return jnp.pad(x, ((0, 0), (0, cols - x.shape[1])))


def layer_kernel(act_ref, cot_ref, wa_ref, wc_ref, go_ref, uo_ref, di_ref, side_ref, a_acc, c_acc):
    k = pl.program_id(0)

    @pl.when(k == 0)
    def _():
        a_acc[...] = jnp.zeros_like(a_acc)
        c_acc[...] = jnp.zeros_like(c_acc)

    f32 = jnp.float32
    a_acc[...] += jnp.dot(act_ref[...], wa_ref[...], preferred_element_type=f32)
    c_acc[...] += jnp.dot(cot_ref[...], wc_ref[...], preferred_element_type=f32)

    @pl.when(k == pl.num_programs(0) - 1)
    def _():
        ff, r = go_ref.shape
        fp = -(-ff // LANE) * LANE
        g = a_acc[:, 0:ff]
        u = a_acc[:, fp : fp + ff]
        b = c_acc[:, 0:ff]
        s = jax.nn.sigmoid(g)
        hidden = (g * s * u).astype(jnp.bfloat16)
        grad_up = (b * g * s).astype(jnp.bfloat16)
        grad_gate = (b * u * s * (1.0 + g * (1.0 - s))).astype(jnp.bfloat16)
        side_ref[:, 0:r] = jnp.dot(grad_gate, go_ref[...], preferred_element_type=f32)
        side_ref[:, r : 2 * r] = jnp.dot(grad_up, uo_ref[...], preferred_element_type=f32)
        side_ref[:, 2 * r : 3 * r] = jnp.dot(hidden, di_ref[...], preferred_element_type=f32)


def layer_call(both, gw, uw, dw, go, uo, di):
    rows, width = both.shape
    d = width // 2
    ff = gw.shape[1]
    r = go.shape[1]
    fp = -(-ff // LANE) * LANE
    wa = jnp.concatenate([pad_to(gw, fp), pad_to(uw, fp)], 1)
    wc = pad_to(dw.T, fp)
    nk = d // KC
    f32 = jnp.float32
    full = lambda shape: pl.BlockSpec(shape, lambda k: (0, 0))
    return pl.pallas_call(
        layer_kernel,
        grid=(nk,),
        in_specs=[
            pl.BlockSpec((rows, KC), lambda k: (0, k)),
            pl.BlockSpec((rows, KC), lambda k: (0, k + nk)),
            pl.BlockSpec((KC, wa.shape[1]), lambda k: (k, 0)),
            pl.BlockSpec((KC, wc.shape[1]), lambda k: (k, 0)),
            full((ff, r)),
            full((ff, r)),
            full((ff, r)),
        ],
        out_specs=full((rows, 3 * r)),
        out_shape=jax.ShapeDtypeStruct((rows, 3 * r), f32),
        scratch_shapes=[
            pltpu.VMEM((rows, wa.shape[1]), f32),
            pltpu.VMEM((rows, wc.shape[1]), f32),
        ],
        compiler_params=pltpu.CompilerParams(
            dimension_semantics=("arbitrary",), vmem_limit_bytes=62 * 1024 * 1024
        ),
        cost_estimate=pl.CostEstimate(
            flops=2 * rows * d * 3 * ff + 2 * rows * ff * 3 * r,
            transcendentals=rows * ff,
            bytes_accessed=2 * (rows * width + d * (wa.shape[1] + wc.shape[1]) + 3 * ff * r) + 4 * rows * 3 * r,
        ),
    )(both, both, wa, wc, go, uo, di)


def scatter_sum(x, n):
    blocks = x.reshape((n, x.shape[0] // n) + x.shape[1:])
    return jnp.sum(lax.all_to_all(blocks, ALL, 0, 0, tiled=False), axis=0)


def gather_rows(x, n):
    copies = jnp.broadcast_to(x[None], (n,) + x.shape)
    got = lax.all_to_all(copies, ALL, 0, 0, tiled=False)
    return got.reshape((n * x.shape[0],) + x.shape[1:])


def body(
    token_ids,
    hidden_in,
    cotangent,
    gate_weight,
    up_weight,
    down_weight,
    gate_in_proj,
    up_in_proj,
    down_out_proj,
    gate_out_proj,
    up_out_proj,
    down_in_proj,
    stored_grads,
    example_ids,
):
    n_all = lax.axis_size("dp") * lax.axis_size("tensor")
    proj_rank = gate_in_proj.shape[1]
    pad_mask = (token_ids != 0).astype(jnp.bfloat16)[:, None]
    masked = cotangent * pad_mask
    both = lax.all_gather(jnp.concatenate([hidden_in, masked], axis=1), "dp", axis=0, tiled=True)
    f32 = jnp.float32
    block = layer_call(both, gate_weight, up_weight, down_weight, gate_out_proj, up_out_proj, down_in_proj)
    summed = gather_rows(scatter_sum(block, n_all), n_all)
    d_model = hidden_in.shape[1]
    in_both = jnp.dot(
        both[:, :d_model], jnp.concatenate([gate_in_proj, up_in_proj], axis=1), preferred_element_type=f32
    )
    in_gate = in_both[:, :proj_rank]
    in_up = in_both[:, proj_rank:]
    out_down = jnp.dot(both[:, d_model:], down_out_proj, preferred_element_type=f32)
    docs = both.shape[0] // LEN

    side_gate = summed[:, :proj_rank]
    side_up = summed[:, proj_rank : 2 * proj_rank]
    side_down = summed[:, 2 * proj_rank :]
    shape = (3, docs, LEN, proj_rank)
    lefts = jnp.stack([in_gate, in_up, side_down]).reshape(shape)
    rights = jnp.stack([side_gate, side_up, out_down]).reshape(shape)
    blocks = jnp.einsum("bdlr,bdls->dbrs", lefts, rights, precision=lax.Precision.HIGHEST)
    all_docs = blocks.reshape(docs, 3 * proj_rank * proj_rank).astype(jnp.bfloat16)
    docs_here = hidden_in.shape[0] // LEN
    doc_grads = lax.dynamic_slice_in_dim(all_docs, lax.axis_index("dp") * docs_here, docs_here, 0)
    examples_all = EX_DEV * n_all
    onehot = (example_ids[:, None] == jnp.arange(examples_all, dtype=jnp.int32)[None, :]).astype(
        jnp.float32
    )
    raw_scores = lax.dot_general(
        all_docs,
        stored_grads,
        (((1,), (1,)), ((), ())),
        preferred_element_type=jnp.float32,
    )
    partial_scores = jnp.dot(raw_scores, onehot, precision=lax.Precision.HIGHEST)
    totals = scatter_sum(partial_scores.T, n_all).T
    return (doc_grads, totals)


def solution(mesh):
    return jax.shard_map(
        body,
        mesh=mesh,
        in_specs=(
            P("dp"),
            P("dp", None),
            P("dp", None),
            P(None, ("dp", "tensor")),
            P(None, ("dp", "tensor")),
            P(("dp", "tensor"), None),
            P(),
            P(),
            P(),
            P(("dp", "tensor"), None),
            P(("dp", "tensor"), None),
            P(("dp", "tensor"), None),
            P(("dp", "tensor"), None),
            P(("dp", "tensor")),
        ),
        out_specs=(P("dp", None), P(None, ("dp", "tensor"))),
        check_vma=False,
    )
```

```python
import jax
import jax.numpy as jnp
from jax import lax
from jax.sharding import PartitionSpec as P

from jax.experimental import pallas as pl
from jax.experimental.pallas import tpu as pltpu

LEN = 32
EX_DEV = 8
ALL = ("dp", "tensor")

KC = 2048
LANE = 128


def pad_to(x, cols):
    return jnp.pad(x, ((0, 0), (0, cols - x.shape[1])))


def layer_kernel(act_ref, cot_ref, wa_ref, wc_ref, go_ref, uo_ref, di_ref, side_ref, a_acc, c_acc):
    k = pl.program_id(0)

    @pl.when(k == 0)
    def _():
        a_acc[...] = jnp.zeros_like(a_acc)
        c_acc[...] = jnp.zeros_like(c_acc)

    f32 = jnp.float32
    a_acc[...] += jnp.dot(act_ref[...], wa_ref[...], preferred_element_type=f32)
    c_acc[...] += jnp.dot(cot_ref[...], wc_ref[...], preferred_element_type=f32)

    @pl.when(k == pl.num_programs(0) - 1)
    def _():
        ff, r = go_ref.shape
        fp = -(-ff // LANE) * LANE
        g = a_acc[:, 0:ff]
        u = a_acc[:, fp : fp + ff]
        b = c_acc[:, 0:ff]
        s = jax.nn.sigmoid(g)
        hidden = (g * s * u).astype(jnp.bfloat16)
        grad_up = (b * g * s).astype(jnp.bfloat16)
        grad_gate = (b * u * s * (1.0 + g * (1.0 - s))).astype(jnp.bfloat16)
        side_ref[:, 0:r] = jnp.dot(grad_gate, go_ref[...], preferred_element_type=f32)
        side_ref[:, r : 2 * r] = jnp.dot(grad_up, uo_ref[...], preferred_element_type=f32)
        side_ref[:, 2 * r : 3 * r] = jnp.dot(hidden, di_ref[...], preferred_element_type=f32)


def layer_call(both, gw, uw, dw, go, uo, di):
    rows, width = both.shape
    d = width // 2
    ff = gw.shape[1]
    r = go.shape[1]
    fp = -(-ff // LANE) * LANE
    wa = jnp.concatenate([pad_to(gw, fp), pad_to(uw, fp)], 1)
    wc = pad_to(dw.T, fp)
    nk = d // KC
    f32 = jnp.float32
    full = lambda shape: pl.BlockSpec(shape, lambda k: (0, 0))
    return pl.pallas_call(
        layer_kernel,
        grid=(nk,),
        in_specs=[
            pl.BlockSpec((rows, KC), lambda k: (0, k)),
            pl.BlockSpec((rows, KC), lambda k: (0, k + nk)),
            pl.BlockSpec((KC, wa.shape[1]), lambda k: (k, 0)),
            pl.BlockSpec((KC, wc.shape[1]), lambda k: (k, 0)),
            full((ff, r)),
            full((ff, r)),
            full((ff, r)),
        ],
        out_specs=full((rows, 3 * r)),
        out_shape=jax.ShapeDtypeStruct((rows, 3 * r), f32),
        scratch_shapes=[
            pltpu.VMEM((rows, wa.shape[1]), f32),
            pltpu.VMEM((rows, wc.shape[1]), f32),
        ],
        compiler_params=pltpu.CompilerParams(
            dimension_semantics=("arbitrary",), vmem_limit_bytes=62 * 1024 * 1024
        ),
        cost_estimate=pl.CostEstimate(
            flops=2 * rows * d * 3 * ff + 2 * rows * ff * 3 * r,
            transcendentals=rows * ff,
            bytes_accessed=2 * (rows * width + d * (wa.shape[1] + wc.shape[1]) + 3 * ff * r) + 4 * rows * 3 * r,
        ),
    )(both, both, wa, wc, go, uo, di)


def ring_perm(n, f):
    return [(i, f(i) % n) for i in range(n)]


def shared_gather(x, n):
    pp = lambda v, p: lax.ppermute(v, "dp", p)
    zp = ring_perm(n, lambda i: i + 4)
    zm = ring_perm(n, lambda i: i - 4)
    yy = ring_perm(n, lambda i: i ^ 2)
    cc = ring_perm(n, lambda i: i ^ 1)
    half = x.shape[0] // 2
    from_zm = pp(x, zp)
    from_zp = pp(x, zm)
    from_y = pp(x, yy)
    o_own = pp(x, cc)
    b_z2 = pp(from_zp, zm)
    b_zm_y = pp(from_y, zp)
    b_zp_y = pp(from_zp, yy)
    o_b = pp(jnp.stack([from_zm, from_zp, from_y]), cc)
    c_z2_y = jnp.concatenate([pp(b_z2[:half], yy), pp(b_zp_y[half:], zm)], axis=0)
    o_c = pp(jnp.stack([b_z2, b_zm_y, b_zp_y]), cc)
    o_d = pp(c_z2_y, cc)
    slots = [x, from_zm, from_zp, from_y, b_z2, b_zm_y, b_zp_y, c_z2_y,
             o_own, o_b[0], o_b[1], o_b[2], o_c[0], o_c[1], o_c[2], o_d]
    d = lax.axis_index("dp")
    mine = [d, d - 4, d + 4, d ^ 2, d + 8, (d - 4) % n ^ 2, (d ^ 2) + 4, (d ^ 2) + 8]
    ids = jnp.stack([m % n for m in mine] + [(m % n) ^ 1 for m in mine])
    return jnp.concatenate(slots, axis=0), jnp.argsort(ids)


def to_dp_order(x, order):
    n = order.shape[0]
    blocks = x.reshape((n, x.shape[0] // n) + x.shape[1:])
    return jnp.take(blocks, order, axis=0).reshape(x.shape)


def scatter_sum(x, n):
    blocks = x.reshape((n, x.shape[0] // n) + x.shape[1:])
    return jnp.sum(lax.all_to_all(blocks, ALL, 0, 0, tiled=False), axis=0)


def gather_rows(x, n):
    copies = jnp.broadcast_to(x[None], (n,) + x.shape)
    got = lax.all_to_all(copies, ALL, 0, 0, tiled=False)
    return got.reshape((n * x.shape[0],) + x.shape[1:])


def body(
    token_ids,
    hidden_in,
    cotangent,
    gate_weight,
    up_weight,
    down_weight,
    gate_in_proj,
    up_in_proj,
    down_out_proj,
    gate_out_proj,
    up_out_proj,
    down_in_proj,
    stored_grads,
    example_ids,
):
    n_all = lax.axis_size("dp") * lax.axis_size("tensor")
    proj_rank = gate_in_proj.shape[1]
    pad_mask = (token_ids != 0).astype(jnp.bfloat16)[:, None]
    masked = cotangent * pad_mask
    both, order = shared_gather(jnp.concatenate([hidden_in, masked], axis=1), lax.axis_size("dp"))
    f32 = jnp.float32
    block = layer_call(both, gate_weight, up_weight, down_weight, gate_out_proj, up_out_proj, down_in_proj)
    summed = gather_rows(scatter_sum(to_dp_order(block, order), n_all), n_all)
    d_model = hidden_in.shape[1]
    in_both = jnp.dot(
        both[:, :d_model], jnp.concatenate([gate_in_proj, up_in_proj], axis=1), preferred_element_type=f32
    )
    in_both = to_dp_order(in_both, order)
    in_gate = in_both[:, :proj_rank]
    in_up = in_both[:, proj_rank:]
    out_down = to_dp_order(jnp.dot(both[:, d_model:], down_out_proj, preferred_element_type=f32), order)
    docs = both.shape[0] // LEN

    side_gate = summed[:, :proj_rank]
    side_up = summed[:, proj_rank : 2 * proj_rank]
    side_down = summed[:, 2 * proj_rank :]
    shape = (3, docs, LEN, proj_rank)
    lefts = jnp.stack([in_gate, in_up, side_down]).reshape(shape)
    rights = jnp.stack([side_gate, side_up, out_down]).reshape(shape)
    blocks = jnp.einsum("bdlr,bdls->dbrs", lefts, rights, precision=lax.Precision.HIGHEST)
    all_docs = blocks.reshape(docs, 3 * proj_rank * proj_rank).astype(jnp.bfloat16)
    docs_here = hidden_in.shape[0] // LEN
    doc_grads = lax.dynamic_slice_in_dim(all_docs, lax.axis_index("dp") * docs_here, docs_here, 0)
    examples_all = EX_DEV * n_all
    onehot = (example_ids[:, None] == jnp.arange(examples_all, dtype=jnp.int32)[None, :]).astype(
        jnp.float32
    )
    raw_scores = lax.dot_general(
        all_docs,
        stored_grads,
        (((1,), (1,)), ((), ())),
        preferred_element_type=jnp.float32,
    )
    partial_scores = jnp.dot(raw_scores, onehot, precision=lax.Precision.HIGHEST)
    totals = scatter_sum(partial_scores.T, n_all).T
    return (doc_grads, totals)


def solution(mesh):
    return jax.shard_map(
        body,
        mesh=mesh,
        in_specs=(
            P("dp"),
            P("dp", None),
            P("dp", None),
            P(None, ("dp", "tensor")),
            P(None, ("dp", "tensor")),
            P(("dp", "tensor"), None),
            P(),
            P(),
            P(),
            P(("dp", "tensor"), None),
            P(("dp", "tensor"), None),
            P(("dp", "tensor"), None),
            P(("dp", "tensor"), None),
            P(("dp", "tensor")),
        ),
        out_specs=(P("dp", None), P(None, ("dp", "tensor"))),
        check_vma=False,
    )
```

```python
import jax
import jax.numpy as jnp
from jax import lax
from jax.sharding import PartitionSpec as P

from jax.experimental import pallas as pl
from jax.experimental.pallas import tpu as pltpu

LEN = 32
EX_DEV = 8
ALL = ("dp", "tensor")

KC = 2048
LANE = 128


def layer_kernel(act_ref, cot_ref, gw_ref, uw_ref, dw_ref, go_ref, uo_ref, di_ref, side_ref, g_acc, u_acc, b_acc):
    k = pl.program_id(0)

    @pl.when(k == 0)
    def _():
        g_acc[...] = jnp.zeros_like(g_acc)
        u_acc[...] = jnp.zeros_like(u_acc)
        b_acc[...] = jnp.zeros_like(b_acc)

    f32 = jnp.float32
    nt = (((1,), (1,)), ((), ()))
    a = act_ref[...]
    g_acc[...] += lax.dot_general(a, gw_ref[...], nt, preferred_element_type=f32)
    u_acc[...] += lax.dot_general(a, uw_ref[...], nt, preferred_element_type=f32)
    b_acc[...] += lax.dot_general(cot_ref[...], dw_ref[...], nt, preferred_element_type=f32)

    @pl.when(k == pl.num_programs(0) - 1)
    def _():
        r = go_ref.shape[1]
        g = g_acc[...]
        u = u_acc[...]
        b = b_acc[...]
        s = jax.nn.sigmoid(g)
        hidden = (g * s * u).astype(jnp.bfloat16)
        grad_up = (b * g * s).astype(jnp.bfloat16)
        grad_gate = (b * u * s * (1.0 + g * (1.0 - s))).astype(jnp.bfloat16)
        side_ref[:, 0:r] = jnp.dot(grad_gate, go_ref[...], preferred_element_type=f32)
        side_ref[:, r : 2 * r] = jnp.dot(grad_up, uo_ref[...], preferred_element_type=f32)
        side_ref[:, 2 * r : 3 * r] = jnp.dot(hidden, di_ref[...], preferred_element_type=f32)


def layer_call(both, gw, uw, dw, go, uo, di):
    rows, width = both.shape
    d = width // 2
    ff, r = go.shape
    nk = d // KC
    f32 = jnp.float32
    full = lambda shape: pl.BlockSpec(shape, lambda k: (0, 0))
    return pl.pallas_call(
        layer_kernel,
        grid=(nk,),
        in_specs=[
            pl.BlockSpec((rows, KC), lambda k: (0, k)),
            pl.BlockSpec((rows, KC), lambda k: (0, k + nk)),
            pl.BlockSpec((ff, KC), lambda k: (0, k)),
            pl.BlockSpec((ff, KC), lambda k: (0, k)),
            pl.BlockSpec((ff, KC), lambda k: (0, k)),
            full((ff, r)),
            full((ff, r)),
            full((ff, r)),
        ],
        out_specs=full((rows, 3 * r)),
        out_shape=jax.ShapeDtypeStruct((rows, 3 * r), f32),
        scratch_shapes=[pltpu.VMEM((rows, ff), f32) for _ in range(3)],
        compiler_params=pltpu.CompilerParams(
            dimension_semantics=("arbitrary",), vmem_limit_bytes=62 * 1024 * 1024
        ),
        cost_estimate=pl.CostEstimate(
            flops=2 * rows * d * 3 * ff + 2 * rows * ff * 3 * r,
            transcendentals=rows * ff,
            bytes_accessed=2 * (rows * width + 3 * d * ff + 3 * ff * r) + 4 * rows * 3 * r,
        ),
    )(both, both, gw.T, uw.T, dw, go, uo, di)


def ring_perm(n, f):
    return [(i, f(i) % n) for i in range(n)]


def shared_gather(x, n):
    pp = lambda v, p: lax.ppermute(v, "dp", p)
    zp = ring_perm(n, lambda i: i + 4)
    zm = ring_perm(n, lambda i: i - 4)
    yy = ring_perm(n, lambda i: i ^ 2)
    cc = ring_perm(n, lambda i: i ^ 1)
    half = x.shape[0] // 2
    from_zm = pp(x, zp)
    from_zp = pp(x, zm)
    from_y = pp(x, yy)
    o_own = pp(x, cc)
    b_z2 = pp(from_zp, zm)
    b_zm_y = pp(from_y, zp)
    b_zp_y = pp(from_zp, yy)
    o_b = pp(jnp.stack([from_zm, from_zp, from_y]), cc)
    c_z2_y = jnp.concatenate([pp(b_z2[:half], yy), pp(b_zp_y[half:], zm)], axis=0)
    o_c = pp(jnp.stack([b_z2, b_zm_y, b_zp_y]), cc)
    o_d = pp(c_z2_y, cc)
    slots = [x, from_zm, from_zp, from_y, b_z2, b_zm_y, b_zp_y, c_z2_y,
             o_own, o_b[0], o_b[1], o_b[2], o_c[0], o_c[1], o_c[2], o_d]
    d = lax.axis_index("dp")
    mine = [d, d - 4, d + 4, d ^ 2, d + 8, (d - 4) % n ^ 2, (d ^ 2) + 4, (d ^ 2) + 8]
    ids = jnp.stack([m % n for m in mine] + [(m % n) ^ 1 for m in mine])
    return jnp.concatenate(slots, axis=0), jnp.argsort(ids)


def to_dp_order(x, order):
    n = order.shape[0]
    blocks = x.reshape((n, x.shape[0] // n) + x.shape[1:])
    return jnp.take(blocks, order, axis=0).reshape(x.shape)


def scatter_sum(x, n):
    blocks = x.reshape((n, x.shape[0] // n) + x.shape[1:])
    return jnp.sum(lax.all_to_all(blocks, ALL, 0, 0, tiled=False), axis=0)


def gather_rows(x, n):
    copies = jnp.broadcast_to(x[None], (n,) + x.shape)
    got = lax.all_to_all(copies, ALL, 0, 0, tiled=False)
    return got.reshape((n * x.shape[0],) + x.shape[1:])


def body(
    token_ids,
    hidden_in,
    cotangent,
    gate_weight,
    up_weight,
    down_weight,
    gate_in_proj,
    up_in_proj,
    down_out_proj,
    gate_out_proj,
    up_out_proj,
    down_in_proj,
    stored_grads,
    example_ids,
):
    n_all = lax.axis_size("dp") * lax.axis_size("tensor")
    proj_rank = gate_in_proj.shape[1]
    pad_mask = (token_ids != 0).astype(jnp.bfloat16)[:, None]
    masked = cotangent * pad_mask
    both, order = shared_gather(jnp.concatenate([hidden_in, masked], axis=1), lax.axis_size("dp"))
    f32 = jnp.float32
    block = layer_call(both, gate_weight, up_weight, down_weight, gate_out_proj, up_out_proj, down_in_proj)
    summed = gather_rows(scatter_sum(to_dp_order(block, order), n_all), n_all)
    d_model = hidden_in.shape[1]
    in_both = jnp.dot(
        both[:, :d_model], jnp.concatenate([gate_in_proj, up_in_proj], axis=1), preferred_element_type=f32
    )
    in_both = to_dp_order(in_both, order)
    in_gate = in_both[:, :proj_rank]
    in_up = in_both[:, proj_rank:]
    out_down = to_dp_order(jnp.dot(both[:, d_model:], down_out_proj, preferred_element_type=f32), order)
    docs = both.shape[0] // LEN

    side_gate = summed[:, :proj_rank]
    side_up = summed[:, proj_rank : 2 * proj_rank]
    side_down = summed[:, 2 * proj_rank :]
    shape = (3, docs, LEN, proj_rank)
    lefts = jnp.stack([in_gate, in_up, side_down]).reshape(shape)
    rights = jnp.stack([side_gate, side_up, out_down]).reshape(shape)
    blocks = jnp.einsum("bdlr,bdls->dbrs", lefts, rights, precision=lax.Precision.HIGHEST)
    all_docs = blocks.reshape(docs, 3 * proj_rank * proj_rank).astype(jnp.bfloat16)
    docs_here = hidden_in.shape[0] // LEN
    doc_grads = lax.dynamic_slice_in_dim(all_docs, lax.axis_index("dp") * docs_here, docs_here, 0)
    examples_all = EX_DEV * n_all
    onehot = (example_ids[:, None] == jnp.arange(examples_all, dtype=jnp.int32)[None, :]).astype(
        jnp.float32
    )
    raw_scores = lax.dot_general(
        all_docs,
        stored_grads,
        (((1,), (1,)), ((), ())),
        preferred_element_type=jnp.float32,
    )
    partial_scores = jnp.dot(raw_scores, onehot, precision=lax.Precision.HIGHEST)
    totals = scatter_sum(partial_scores.T, n_all).T
    return (doc_grads, totals)


def solution(mesh):
    return jax.shard_map(
        body,
        mesh=mesh,
        in_specs=(
            P("dp"),
            P("dp", None),
            P("dp", None),
            P(None, ("dp", "tensor")),
            P(None, ("dp", "tensor")),
            P(("dp", "tensor"), None),
            P(),
            P(),
            P(),
            P(("dp", "tensor"), None),
            P(("dp", "tensor"), None),
            P(("dp", "tensor"), None),
            P(("dp", "tensor"), None),
            P(("dp", "tensor")),
        ),
        out_specs=(P("dp", None), P(None, ("dp", "tensor"))),
        check_vma=False,
    )
```

```python
import jax
import jax.numpy as jnp
from jax import lax
from jax.sharding import PartitionSpec as P

from jax.experimental import pallas as pl
from jax.experimental.pallas import tpu as pltpu

LEN = 32
EX_DEV = 8
ALL = ("dp", "tensor")

KC = 2048
LANE = 128


def layer_kernel(act_ref, cot_ref, gw_ref, uw_ref, dw_ref, go_ref, uo_ref, di_ref, side_ref, g_acc, u_acc, b_acc):
    k = pl.program_id(0)

    @pl.when(k == 0)
    def _():
        g_acc[...] = jnp.zeros_like(g_acc)
        u_acc[...] = jnp.zeros_like(u_acc)
        b_acc[...] = jnp.zeros_like(b_acc)

    f32 = jnp.float32
    nt = (((1,), (1,)), ((), ()))
    a = act_ref[...]
    g_acc[...] += lax.dot_general(a, gw_ref[...], nt, preferred_element_type=f32)
    u_acc[...] += lax.dot_general(a, uw_ref[...], nt, preferred_element_type=f32)
    b_acc[...] += lax.dot_general(cot_ref[...], dw_ref[...], nt, preferred_element_type=f32)

    @pl.when(k == pl.num_programs(0) - 1)
    def _():
        r = go_ref.shape[1]
        g = g_acc[...]
        u = u_acc[...]
        b = b_acc[...]
        s = jax.nn.sigmoid(g)
        hidden = (g * s * u).astype(jnp.bfloat16)
        grad_up = (b * g * s).astype(jnp.bfloat16)
        grad_gate = (b * u * s * (1.0 + g * (1.0 - s))).astype(jnp.bfloat16)
        side_ref[:, 0:r] = jnp.dot(grad_gate, go_ref[...], preferred_element_type=f32)
        side_ref[:, r : 2 * r] = jnp.dot(grad_up, uo_ref[...], preferred_element_type=f32)
        side_ref[:, 2 * r : 3 * r] = jnp.dot(hidden, di_ref[...], preferred_element_type=f32)


def layer_call(both, gw, uw, dw, go, uo, di):
    rows, width = both.shape
    d = width // 2
    ff, r = go.shape
    nk = d // KC
    f32 = jnp.float32
    full = lambda shape: pl.BlockSpec(shape, lambda k: (0, 0))
    return pl.pallas_call(
        layer_kernel,
        grid=(nk,),
        in_specs=[
            pl.BlockSpec((rows, KC), lambda k: (0, k)),
            pl.BlockSpec((rows, KC), lambda k: (0, k + nk)),
            pl.BlockSpec((ff, KC), lambda k: (0, k)),
            pl.BlockSpec((ff, KC), lambda k: (0, k)),
            pl.BlockSpec((ff, KC), lambda k: (0, k)),
            full((ff, r)),
            full((ff, r)),
            full((ff, r)),
        ],
        out_specs=full((rows, 3 * r)),
        out_shape=jax.ShapeDtypeStruct((rows, 3 * r), f32),
        scratch_shapes=[pltpu.VMEM((rows, ff), f32) for _ in range(3)],
        compiler_params=pltpu.CompilerParams(
            dimension_semantics=("arbitrary",), vmem_limit_bytes=62 * 1024 * 1024
        ),
        cost_estimate=pl.CostEstimate(
            flops=2 * rows * d * 3 * ff + 2 * rows * ff * 3 * r,
            transcendentals=rows * ff,
            bytes_accessed=2 * (rows * width + 3 * d * ff + 3 * ff * r) + 4 * rows * 3 * r,
        ),
    )(both, both, gw.T, uw.T, dw, go, uo, di)


def ring_perm(n, f):
    return [(i, f(i) % n) for i in range(n)]


def shared_gather(x, n):
    pp = lambda v, p: lax.ppermute(v, "dp", p)
    zp = ring_perm(n, lambda i: i + 4)
    zm = ring_perm(n, lambda i: i - 4)
    yy = ring_perm(n, lambda i: i ^ 2)
    cc = ring_perm(n, lambda i: i ^ 1)
    from_zm = pp(x, zp)
    from_zp = pp(x, zm)
    from_y = pp(x, yy)
    o_own = pp(x, cc)
    b_z2 = pp(from_zp, zm)
    b_zm_y = pp(from_y, zp)
    b_zp_y = pp(from_zp, yy)
    o_b = pp(jnp.stack([from_zm, from_zp, from_y]), cc)
    third = (x.shape[1] // 3) // 128 * 128
    c_z2_y = jnp.concatenate(
        [
            pp(b_z2[:, :third], yy),
            pp(b_zp_y[:, third : 2 * third], zm),
            pp(b_zm_y[:, 2 * third :], zp),
        ],
        axis=1,
    )
    o_c = pp(jnp.stack([b_z2, b_zm_y, b_zp_y]), cc)
    o_d = pp(c_z2_y, cc)
    slots = [x, from_zm, from_zp, from_y, b_z2, b_zm_y, b_zp_y, c_z2_y,
             o_own, o_b[0], o_b[1], o_b[2], o_c[0], o_c[1], o_c[2], o_d]
    d = lax.axis_index("dp")
    mine = [d, d - 4, d + 4, d ^ 2, d + 8, (d - 4) % n ^ 2, (d ^ 2) + 4, (d ^ 2) + 8]
    ids = jnp.stack([m % n for m in mine] + [(m % n) ^ 1 for m in mine])
    return jnp.concatenate(slots, axis=0), jnp.argsort(ids)


def to_dp_order(x, order):
    n = order.shape[0]
    blocks = x.reshape((n, x.shape[0] // n) + x.shape[1:])
    return jnp.take(blocks, order, axis=0).reshape(x.shape)


def scatter_sum(x, n):
    blocks = x.reshape((n, x.shape[0] // n) + x.shape[1:])
    return jnp.sum(lax.all_to_all(blocks, ALL, 0, 0, tiled=False), axis=0)


def gather_rows(x, n):
    copies = jnp.broadcast_to(x[None], (n,) + x.shape)
    got = lax.all_to_all(copies, ALL, 0, 0, tiled=False)
    return got.reshape((n * x.shape[0],) + x.shape[1:])


def body(
    token_ids,
    hidden_in,
    cotangent,
    gate_weight,
    up_weight,
    down_weight,
    gate_in_proj,
    up_in_proj,
    down_out_proj,
    gate_out_proj,
    up_out_proj,
    down_in_proj,
    stored_grads,
    example_ids,
):
    n_all = lax.axis_size("dp") * lax.axis_size("tensor")
    proj_rank = gate_in_proj.shape[1]
    pad_mask = (token_ids != 0).astype(jnp.bfloat16)[:, None]
    masked = cotangent * pad_mask
    both, order = shared_gather(jnp.concatenate([hidden_in, masked], axis=1), lax.axis_size("dp"))
    f32 = jnp.float32
    block = layer_call(both, gate_weight, up_weight, down_weight, gate_out_proj, up_out_proj, down_in_proj)
    summed = gather_rows(scatter_sum(to_dp_order(block, order), n_all), n_all)
    d_model = hidden_in.shape[1]
    in_both = jnp.dot(
        both[:, :d_model], jnp.concatenate([gate_in_proj, up_in_proj], axis=1), preferred_element_type=f32
    )
    in_both = to_dp_order(in_both, order)
    in_gate = in_both[:, :proj_rank]
    in_up = in_both[:, proj_rank:]
    out_down = to_dp_order(jnp.dot(both[:, d_model:], down_out_proj, preferred_element_type=f32), order)
    docs = both.shape[0] // LEN

    side_gate = summed[:, :proj_rank]
    side_up = summed[:, proj_rank : 2 * proj_rank]
    side_down = summed[:, 2 * proj_rank :]
    shape = (3, docs, LEN, proj_rank)
    lefts = jnp.stack([in_gate, in_up, side_down]).reshape(shape)
    rights = jnp.stack([side_gate, side_up, out_down]).reshape(shape)
    blocks = jnp.einsum("bdlr,bdls->dbrs", lefts, rights, precision=lax.Precision.HIGHEST)
    all_docs = blocks.reshape(docs, 3 * proj_rank * proj_rank).astype(jnp.bfloat16)
    docs_here = hidden_in.shape[0] // LEN
    doc_grads = lax.dynamic_slice_in_dim(all_docs, lax.axis_index("dp") * docs_here, docs_here, 0)
    examples_all = EX_DEV * n_all
    onehot = (example_ids[:, None] == jnp.arange(examples_all, dtype=jnp.int32)[None, :]).astype(
        jnp.float32
    )
    raw_scores = lax.dot_general(
        all_docs,
        stored_grads,
        (((1,), (1,)), ((), ())),
        preferred_element_type=jnp.float32,
    )
    partial_scores = jnp.dot(raw_scores, onehot, precision=lax.Precision.HIGHEST)
    totals = scatter_sum(partial_scores.T, n_all).T
    return (doc_grads, totals)


def solution(mesh):
    return jax.shard_map(
        body,
        mesh=mesh,
        in_specs=(
            P("dp"),
            P("dp", None),
            P("dp", None),
            P(None, ("dp", "tensor")),
            P(None, ("dp", "tensor")),
            P(("dp", "tensor"), None),
            P(),
            P(),
            P(),
            P(("dp", "tensor"), None),
            P(("dp", "tensor"), None),
            P(("dp", "tensor"), None),
            P(("dp", "tensor"), None),
            P(("dp", "tensor")),
        ),
        out_specs=(P("dp", None), P(None, ("dp", "tensor"))),
        check_vma=False,
    )
```

```python
import jax
import jax.numpy as jnp
from jax import lax
from jax.sharding import PartitionSpec as P

from jax.experimental import pallas as pl
from jax.experimental.pallas import tpu as pltpu

LEN = 32
EX_DEV = 8
ALL = ("dp", "tensor")

KC = 2048
LANE = 128


def layer_kernel(act_ref, cot_ref, gw_ref, uw_ref, dw_ref, go_ref, uo_ref, di_ref, side_ref, g_acc, u_acc, b_acc):
    k = pl.program_id(0)

    @pl.when(k == 0)
    def _():
        g_acc[...] = jnp.zeros_like(g_acc)
        u_acc[...] = jnp.zeros_like(u_acc)
        b_acc[...] = jnp.zeros_like(b_acc)

    f32 = jnp.float32
    nt = (((1,), (1,)), ((), ()))
    a = act_ref[...]
    g_acc[...] += lax.dot_general(a, gw_ref[...], nt, preferred_element_type=f32)
    u_acc[...] += lax.dot_general(a, uw_ref[...], nt, preferred_element_type=f32)
    b_acc[...] += lax.dot_general(cot_ref[...], dw_ref[...], nt, preferred_element_type=f32)

    @pl.when(k == pl.num_programs(0) - 1)
    def _():
        r = go_ref.shape[1]
        g = g_acc[...]
        u = u_acc[...]
        b = b_acc[...]
        s = jax.nn.sigmoid(g)
        hidden = (g * s * u).astype(jnp.bfloat16)
        grad_up = (b * g * s).astype(jnp.bfloat16)
        grad_gate = (b * u * s * (1.0 + g * (1.0 - s))).astype(jnp.bfloat16)
        side_ref[:, 0:r] = jnp.dot(grad_gate, go_ref[...], preferred_element_type=f32)
        side_ref[:, r : 2 * r] = jnp.dot(grad_up, uo_ref[...], preferred_element_type=f32)
        side_ref[:, 2 * r : 3 * r] = jnp.dot(hidden, di_ref[...], preferred_element_type=f32)


def layer_call(both, gw, uw, dw, go, uo, di):
    rows, width = both.shape
    d = width // 2
    ff, r = go.shape
    nk = d // KC
    f32 = jnp.float32
    full = lambda shape: pl.BlockSpec(shape, lambda k: (0, 0))
    return pl.pallas_call(
        layer_kernel,
        grid=(nk,),
        in_specs=[
            pl.BlockSpec((rows, KC), lambda k: (0, k)),
            pl.BlockSpec((rows, KC), lambda k: (0, k + nk)),
            pl.BlockSpec((ff, KC), lambda k: (0, k)),
            pl.BlockSpec((ff, KC), lambda k: (0, k)),
            pl.BlockSpec((ff, KC), lambda k: (0, k)),
            full((ff, r)),
            full((ff, r)),
            full((ff, r)),
        ],
        out_specs=full((rows, 3 * r)),
        out_shape=jax.ShapeDtypeStruct((rows, 3 * r), f32),
        scratch_shapes=[pltpu.VMEM((rows, ff), f32) for _ in range(3)],
        compiler_params=pltpu.CompilerParams(
            dimension_semantics=("arbitrary",), vmem_limit_bytes=62 * 1024 * 1024
        ),
        cost_estimate=pl.CostEstimate(
            flops=2 * rows * d * 3 * ff + 2 * rows * ff * 3 * r,
            transcendentals=rows * ff,
            bytes_accessed=2 * (rows * width + 3 * d * ff + 3 * ff * r) + 4 * rows * 3 * r,
        ),
    )(both, both, gw.T, uw.T, dw, go, uo, di)


def ring_perm(n, f):
    return [(i, f(i) % n) for i in range(n)]


def shared_gather(x, n):
    pp = lambda v, p: lax.ppermute(v, "dp", p)
    zp = ring_perm(n, lambda i: i + 4)
    zm = ring_perm(n, lambda i: i - 4)
    yy = ring_perm(n, lambda i: i ^ 2)
    cc = ring_perm(n, lambda i: i ^ 1)
    from_zm = pp(x, zp)
    from_zp = pp(x, zm)
    from_y = pp(x, yy)
    o_own = pp(x, cc)
    b_z2 = pp(from_zp, zm)
    b_zm_y = pp(from_y, zp)
    b_zp_y = pp(from_zp, yy)
    o_b = pp(jnp.stack([from_zm, from_zp, from_y]), cc)
    third = (x.shape[1] // 3) // 128 * 128
    c_z2_y = jnp.concatenate(
        [
            pp(b_z2[:, :third], yy),
            pp(b_zp_y[:, third : 2 * third], zm),
            pp(b_zm_y[:, 2 * third :], zp),
        ],
        axis=1,
    )
    o_c = pp(jnp.stack([b_z2, b_zm_y, b_zp_y]), cc)
    o_d = pp(c_z2_y, cc)
    slots = [x, from_zm, from_zp, from_y, b_z2, b_zm_y, b_zp_y, c_z2_y,
             o_own, o_b[0], o_b[1], o_b[2], o_c[0], o_c[1], o_c[2], o_d]
    d = lax.axis_index("dp")
    mine = [d, d - 4, d + 4, d ^ 2, d + 8, (d - 4) % n ^ 2, (d ^ 2) + 4, (d ^ 2) + 8]
    ids = jnp.stack([m % n for m in mine] + [(m % n) ^ 1 for m in mine])
    first = [0, 1, 2, 3, 4, 5, 6, 8, 9, 10, 11]
    last = [7, 12, 13, 14, 15]
    early = jnp.concatenate([slots[i] for i in first], axis=0)
    late = jnp.concatenate([slots[i] for i in last], axis=0)
    return early, late, jnp.argsort(ids[jnp.array(first + last)])


def to_dp_order(x, order):
    n = order.shape[0]
    blocks = x.reshape((n, x.shape[0] // n) + x.shape[1:])
    return jnp.take(blocks, order, axis=0).reshape(x.shape)


def scatter_sum(x, n):
    blocks = x.reshape((n, x.shape[0] // n) + x.shape[1:])
    return jnp.sum(lax.all_to_all(blocks, ALL, 0, 0, tiled=False), axis=0)


def gather_rows(x, n):
    copies = jnp.broadcast_to(x[None], (n,) + x.shape)
    got = lax.all_to_all(copies, ALL, 0, 0, tiled=False)
    return got.reshape((n * x.shape[0],) + x.shape[1:])


def body(
    token_ids,
    hidden_in,
    cotangent,
    gate_weight,
    up_weight,
    down_weight,
    gate_in_proj,
    up_in_proj,
    down_out_proj,
    gate_out_proj,
    up_out_proj,
    down_in_proj,
    stored_grads,
    example_ids,
):
    n_all = lax.axis_size("dp") * lax.axis_size("tensor")
    proj_rank = gate_in_proj.shape[1]
    pad_mask = (token_ids != 0).astype(jnp.bfloat16)[:, None]
    masked = cotangent * pad_mask
    early, late, order = shared_gather(jnp.concatenate([hidden_in, masked], axis=1), lax.axis_size("dp"))
    f32 = jnp.float32
    weights = (gate_weight, up_weight, down_weight, gate_out_proj, up_out_proj, down_in_proj)
    block = jnp.concatenate([layer_call(early, *weights), layer_call(late, *weights)], axis=0)
    summed = gather_rows(scatter_sum(to_dp_order(block, order), n_all), n_all)
    d_model = hidden_in.shape[1]
    in_proj = jnp.concatenate([gate_in_proj, up_in_proj], axis=1)
    in_both = jnp.concatenate(
        [jnp.dot(rows[:, :d_model], in_proj, preferred_element_type=f32) for rows in (early, late)], axis=0
    )
    in_both = to_dp_order(in_both, order)
    in_gate = in_both[:, :proj_rank]
    in_up = in_both[:, proj_rank:]
    out_down = jnp.concatenate(
        [jnp.dot(rows[:, d_model:], down_out_proj, preferred_element_type=f32) for rows in (early, late)], axis=0
    )
    out_down = to_dp_order(out_down, order)
    docs = (early.shape[0] + late.shape[0]) // LEN

    side_gate = summed[:, :proj_rank]
    side_up = summed[:, proj_rank : 2 * proj_rank]
    side_down = summed[:, 2 * proj_rank :]
    shape = (3, docs, LEN, proj_rank)
    lefts = jnp.stack([in_gate, in_up, side_down]).reshape(shape)
    rights = jnp.stack([side_gate, side_up, out_down]).reshape(shape)
    blocks = jnp.einsum("bdlr,bdls->dbrs", lefts, rights, precision=lax.Precision.HIGHEST)
    all_docs = blocks.reshape(docs, 3 * proj_rank * proj_rank).astype(jnp.bfloat16)
    docs_here = hidden_in.shape[0] // LEN
    doc_grads = lax.dynamic_slice_in_dim(all_docs, lax.axis_index("dp") * docs_here, docs_here, 0)
    examples_all = EX_DEV * n_all
    onehot = (example_ids[:, None] == jnp.arange(examples_all, dtype=jnp.int32)[None, :]).astype(
        jnp.float32
    )
    raw_scores = lax.dot_general(
        all_docs,
        stored_grads,
        (((1,), (1,)), ((), ())),
        preferred_element_type=jnp.float32,
    )
    partial_scores = jnp.dot(raw_scores, onehot, precision=lax.Precision.HIGHEST)
    totals = scatter_sum(partial_scores.T, n_all).T
    return (doc_grads, totals)


def solution(mesh):
    return jax.shard_map(
        body,
        mesh=mesh,
        in_specs=(
            P("dp"),
            P("dp", None),
            P("dp", None),
            P(None, ("dp", "tensor")),
            P(None, ("dp", "tensor")),
            P(("dp", "tensor"), None),
            P(),
            P(),
            P(),
            P(("dp", "tensor"), None),
            P(("dp", "tensor"), None),
            P(("dp", "tensor"), None),
            P(("dp", "tensor"), None),
            P(("dp", "tensor")),
        ),
        out_specs=(P("dp", None), P(None, ("dp", "tensor"))),
        check_vma=False,
    )
```
